128 devices in a mesh: seq: 16 (over x_hi, z, core), tp: 8 (over y, x_lo).
Axes of the slice: x: 4 (x_hi: 2, x_lo: 2; x = x_hi * 2 + x_lo), y: 4, z: 4, core: 2. Of those that a mesh axis runs over, the one named last changes fastest.
Arguments:
- tokens: bfloat16 [4, 2048, 4096], P(None, 'seq', 'tp'), may hold values from -6 to 6
- new_tokens: bfloat16 [4, 4096], P(None, 'tp'), may hold values from -6 to 6
- w_qkv: bfloat16 [3, 4096, 4096], P(None, None, 'tp')
- w_out: bfloat16 [4096, 4096], P('tp')
- q_gain: float32 [4096], P('tp'), may hold values from 0.5 to 6
- k_gain: float32 [4096], P('tp'), may hold values from 0.5 to 6
- post_gain: float32 [4096], P('tp'), may hold values from 0.5 to 1.5
- lengths: int32 [4], replicated, may hold values from 1 to 2048, 6144 in all
Outputs:
- hidden_out: bfloat16 [4, 2048, 4096], P(None, 'seq', 'tp')
- new_out: bfloat16 [4, 4096], P(None, 'tp')
The draws below stay inside these ranges and needn't reach their ends.
Inputs may be any that keep to these rules, and one draw needn't show every extreme that they name: `lengths`: one prompt has exactly 2048 live tokens.
All inputs are finite; a program needn't handle non-finite values.
Results may differ from the reference program's by a relative error of at most 0.012.
The reference program's roundings to bfloat16 on the way (of `value` and `attention`) count: a program that leaves them out, or rounds other values in their place, can miss the bound.
Values may be sent and summed in bfloat16 or wider, within the bound.
No kernel may reach another device: no remote copies, remote signals or barrier semaphores. Data moves between devices by JAX's collectives and lax.ppermute only.
A program may use at most 128 MiB of HBM per device.

```python
import math
import jax
import jax.numpy as jnp
import numpy as np
from jax import lax

D = 4096
HEADS = 32
HD = 128
SEQS = 4
LEN = 2048


def column_scale(size):
    return 0.5 + 1.5 * jnp.arange(size, dtype=jnp.float32) / size


def weight_base(key, shape):
    base = jax.random.normal(key, shape, jnp.float32)
    return base


def draw_w_qkv(key, part):
    base = weight_base(jax.random.fold_in(key, 11), (3, D, D))
    return (base * D ** (-0.5) * column_scale(D)).astype(jnp.bfloat16)


def draw_w_out(key, part):
    base = weight_base(jax.random.fold_in(key, 23), (D, D))
    return (base * D ** (-0.5) * column_scale(D)).astype(jnp.bfloat16)


def gain_draw(key, salt):
    uniform_part = jax.random.uniform(jax.random.fold_in(key, salt), (D,), jnp.float32)
    lower, upper = (0.5, 2.0)
    return jnp.exp(math.log(lower) + uniform_part * (math.log(upper) - math.log(lower)))


def draw_q_gain(key, part):
    return gain_draw(key, 37)


def draw_k_gain(key, part):
    return gain_draw(key, 41)


def steps_of(stream_key, extent, shards, least, largest):
    def one(dim, blocks):
        draws = jax.random.uniform(jax.random.fold_in(jax.random.fold_in(stream_key, 6), dim), (blocks,), jnp.float32, least / len(shards), largest / len(shards))
        return jnp.repeat(jnp.exp(draws), extent[dim] // blocks).reshape((-1,) + (1,) * (len(extent) - dim - 1))

    factor_of = one(*shards[0])
    for cut in shards[1:]:
        factor_of = factor_of * one(*cut)
    return factor_of


def length_profile(number_of, total, bound, skew):
    loads = [(1 << 20) // math.isqrt(rank ** skew) + 1 for rank in range(2, number_of + 1)]
    rest, counts = total - bound - (number_of - 1), [1] * (number_of - 1)
    while rest > 0:
        free = [i for i in range(number_of - 1) if counts[i] < bound]
        mass, left = sum([loads[i] for i in free]), rest
        for i in free:
            extra = min(bound - counts[i], max(1, left * loads[i] // mass), rest)
            counts[i] = counts[i] + extra
            rest = rest - extra
    return np.array([bound] + counts)


def uneven_parts(stream_key, number_of, total, most, slope):
    if number_of == 2:
        one = jax.random.randint(stream_key, (), max(1, total - most), min(most, total - 1) + 1)
        return jnp.stack([one, total - one])
    tallies = jnp.asarray(length_profile(number_of, total, most, slope), jnp.int32)
    couples = (number_of - 1) // 2
    giver, sink = tallies[1:1 + 2 * couples:2], tallies[2:2 + 2 * couples:2]
    room = jnp.minimum(giver - 1, most - sink)
    moved = jax.random.randint(jax.random.fold_in(stream_key, 1), (couples,), 0, 1 << 20) % (room + 1)
    tallies = tallies.at[1:1 + 2 * couples:2].set(giver - moved).at[2:2 + 2 * couples:2].set(sink + moved)
    return tallies[jax.random.permutation(jax.random.fold_in(stream_key, 2), number_of)]


def noise(rng, shape, scale, limit, pieces=(), held_as=jnp.bfloat16):
    values = jax.random.normal(rng, shape, jnp.float32) * scale
    if len(pieces) > 0:
        values = steps_of(rng, shape, pieces, -0.22, 0.18) * values
    return jnp.clip(values, min=-limit, max=limit).astype(held_as)


def setup_inputs(seed: int = 0) -> dict:
    seeds = jax.random.split(jax.random.key(seed), 9)
    return {
        "tokens": noise(seeds[0], (SEQS, LEN, D), 1.0, 6.0, ((1, 16), (2, 8))),
        "new_tokens": noise(seeds[1], (SEQS, D), 1.0, 6.0, ((1, 8),)),
        "w_qkv": draw_w_qkv(jax.random.fold_in(seeds[8], 71), 0),
        "w_out": draw_w_out(jax.random.fold_in(seeds[8], 71), 0),
        "q_gain": draw_q_gain(jax.random.fold_in(seeds[8], 71), 0),
        "k_gain": draw_k_gain(jax.random.fold_in(seeds[8], 71), 0),
        "post_gain": jnp.clip(1.0 + 0.1 * jax.random.normal(seeds[6], (D,), jnp.float32), 0.5, 1.5),
        "lengths": uneven_parts(seeds[7], SEQS, 3 * LEN, LEN, 1).astype(jnp.int32),
    }


rope_base = 500000.0
norm_eps = 1e-06
masked_fill = -1e+30

def rotate(values, position):
    half = values.shape[-1] // 2
    freq = rope_base ** (-(jnp.arange(half, dtype=jnp.float32) * 2.0) / values.shape[-1])
    angle = position.astype(jnp.float32)[..., None] * freq
    cosine = jnp.cos(angle)
    sine = jnp.sin(angle)
    lower = values[..., :half]
    upper = values[..., half:]
    return jnp.concatenate([lower * cosine - upper * sine, upper * cosine + lower * sine], -1)

def rms_scaled(values, gain):
    return values * lax.rsqrt(lax.optimization_barrier(jnp.mean(values * values, -1, keepdims=True)) + norm_eps) * gain

def attend_one(item):
    query_all, key_all, value_all, query_new, key_new, value_new, length = item
    scale = HD ** (-0.5)
    scores = jnp.dot(query_all, key_all.T, preferred_element_type=jnp.float32) * scale
    query_pos = jnp.arange(LEN, dtype=jnp.int32)[:, None]
    key_pos = jnp.arange(LEN, dtype=jnp.int32)[None, :]
    valid = (key_pos <= query_pos) & (key_pos < length)
    scores = jnp.where(valid, scores, masked_fill)
    top = lax.optimization_barrier(jnp.max(scores, -1, keepdims=True))
    weights = jnp.where(valid, jnp.exp(scores - top), 0.0)
    total = lax.optimization_barrier(jnp.sum(weights, -1, keepdims=True))
    prompt_out = jnp.dot(weights.astype(jnp.bfloat16), value_all, preferred_element_type=jnp.float32) / total
    new_scores = jnp.dot(key_all, query_new, preferred_element_type=jnp.float32) * scale
    live = jnp.arange(LEN, dtype=jnp.int32) < length
    new_scores = jnp.where(live, new_scores, masked_fill)
    self_score = jnp.dot(query_new, key_new, preferred_element_type=jnp.float32) * scale
    new_top = jnp.maximum(jnp.max(new_scores), self_score)
    new_weights = jnp.where(live, jnp.exp(new_scores - new_top), 0.0)
    own_weight = jnp.exp(self_score - new_top)
    new_total = jnp.sum(new_weights) + own_weight
    own_rounded = lax.optimization_barrier(own_weight.astype(jnp.bfloat16)).astype(jnp.float32)
    numer = jnp.dot(new_weights.astype(jnp.bfloat16), value_all, preferred_element_type=jnp.float32)
    numer = numer + own_rounded * value_new.astype(jnp.float32)
    return (prompt_out.astype(jnp.bfloat16), (numer / new_total).astype(jnp.bfloat16))

def reference(tokens, new_tokens, w_qkv, w_out, q_gain, k_gain, post_gain, lengths):
    prompt_rows = SEQS * LEN
    rows = jnp.concatenate([tokens.reshape(prompt_rows, D), new_tokens], 0)
    query_raw = jnp.dot(rows, w_qkv[0], preferred_element_type=jnp.float32)
    key_raw = jnp.dot(rows, w_qkv[1], preferred_element_type=jnp.float32)
    value = jnp.dot(rows, w_qkv[2], preferred_element_type=jnp.float32).astype(jnp.bfloat16)
    position = jnp.concatenate([jnp.tile(jnp.arange(LEN, dtype=jnp.int32), SEQS), lengths.astype(jnp.int32)], 0)
    query = rotate(rms_scaled(query_raw, q_gain).reshape(-1, HEADS, HD), position[:, None]).astype(jnp.bfloat16)
    key = rotate(rms_scaled(key_raw, k_gain).reshape(-1, HEADS, HD), position[:, None]).astype(jnp.bfloat16)
    value = value.reshape(-1, HEADS, HD)

    def by_head(array):
        return array[:prompt_rows].reshape(SEQS, LEN, HEADS, HD).transpose(0, 2, 1, 3).reshape(SEQS * HEADS, LEN, HD)

    def new_head(array):
        return array[prompt_rows:].reshape(SEQS * HEADS, HD)
    head_lengths = jnp.repeat(lengths.astype(jnp.int32), HEADS)
    prompt_attn, new_attn = lax.map(attend_one, (by_head(query), by_head(key), by_head(value), new_head(query), new_head(key), new_head(value), head_lengths))
    prompt_attn = prompt_attn.reshape(SEQS, HEADS, LEN, HD).transpose(0, 2, 1, 3).reshape(prompt_rows, D)
    new_attn = new_attn.reshape(SEQS, D)
    attention = jnp.concatenate([prompt_attn, new_attn], 0)
    projected = jnp.dot(attention, w_out, preferred_element_type=jnp.float32)
    result = (rows.astype(jnp.float32) + rms_scaled(projected, post_gain)).astype(jnp.bfloat16)
    return (result[:prompt_rows].reshape(SEQS, LEN, D), result[prompt_rows:])
```

```python
import jax
import jax.numpy as jnp
from jax import lax
from jax.sharding import PartitionSpec as P

HD = 128


rope_base = 500000.0
norm_eps = 1e-06
masked_fill = -1e30


def rotate(values, position):
    half = values.shape[-1] // 2
    freq = rope_base ** (-(jnp.arange(half, dtype=jnp.float32) * 2.0) / values.shape[-1])
    angle = position.astype(jnp.float32)[..., None] * freq
    cosine = jnp.cos(angle)
    sine = jnp.sin(angle)
    lower = values[..., :half]
    upper = values[..., half:]
    return jnp.concatenate([lower * cosine - upper * sine, upper * cosine + lower * sine], -1)


def attend_pair(q_all, k_all, v_all, q_new, k_new, v_new, length):
    count = q_all.shape[0]
    scale = HD ** (-0.5)
    scores = jnp.dot(q_all, k_all.T, preferred_element_type=jnp.float32) * scale
    query_pos = jnp.arange(count, dtype=jnp.int32)[:, None]
    key_pos = jnp.arange(count, dtype=jnp.int32)[None, :]
    valid = (key_pos <= query_pos) & (key_pos < length)
    scores = jnp.where(valid, scores, masked_fill)
    top = jnp.max(scores, -1, keepdims=True)
    weights = jnp.where(valid, jnp.exp(scores - top), 0.0)
    total = jnp.sum(weights, -1, keepdims=True)
    prompt_out = (
        jnp.dot(weights.astype(jnp.bfloat16), v_all, preferred_element_type=jnp.float32) / total
    ).astype(jnp.bfloat16)
    new_scores = jnp.dot(k_all, q_new, preferred_element_type=jnp.float32) * scale
    live = jnp.arange(count, dtype=jnp.int32) < length
    new_scores = jnp.where(live, new_scores, masked_fill)
    self_score = jnp.dot(q_new, k_new, preferred_element_type=jnp.float32) * scale
    new_top = jnp.maximum(jnp.max(new_scores), self_score)
    new_weights = jnp.where(live, jnp.exp(new_scores - new_top), 0.0)
    own_weight = jnp.exp(self_score - new_top)
    new_total = jnp.sum(new_weights) + own_weight
    own_rounded = lax.optimization_barrier(own_weight.astype(jnp.bfloat16)).astype(jnp.float32)
    numer = jnp.dot(new_weights.astype(jnp.bfloat16), v_all, preferred_element_type=jnp.float32)
    numer = numer + own_rounded * v_new.astype(jnp.float32)
    return prompt_out, (numer / new_total).astype(jnp.bfloat16)


def body(tokens, new_tokens, w_qkv, w_out, q_gain, k_gain, post_gain, lengths):
    seqs, pos_dev, width_local = tokens.shape
    heads_local = width_local // HD
    full_width = w_qkv.shape[1]
    n_seq = lax.axis_size("seq")
    pairs = seqs * heads_local
    assert pairs == n_seq
    prompt_rows = seqs * pos_dev
    full_len = pos_dev * n_seq
    flat_rows = tokens.reshape(prompt_rows, width_local)
    local_rows = jnp.concatenate([flat_rows, new_tokens], 0)
    all_rows = lax.all_gather(local_rows, "tp", axis=1, tiled=True)
    proj = jnp.einsum("tn,cnf->ctf", all_rows, w_qkv, preferred_element_type=jnp.float32)
    query_raw, key_raw = proj[0], proj[1]
    query_sq, key_sq = lax.psum(
        (jnp.sum(query_raw * query_raw, -1), jnp.sum(key_raw * key_raw, -1)), "tp"
    )

    def normed(values, square_sum, gain):
        return values * lax.rsqrt(square_sum[:, None] / full_width + norm_eps) * gain

    seq_index = lax.axis_index("seq")
    query_pos = seq_index * pos_dev + jnp.arange(pos_dev, dtype=jnp.int32)
    row_pos = jnp.concatenate([jnp.tile(query_pos, seqs), lengths.astype(jnp.int32)], 0)
    rows_all = prompt_rows + seqs
    queries = rotate(
        normed(query_raw, query_sq, q_gain).reshape(rows_all, heads_local, HD), row_pos[:, None]
    ).astype(jnp.bfloat16)
    keys = rotate(
        normed(key_raw, key_sq, k_gain).reshape(rows_all, heads_local, HD), row_pos[:, None]
    ).astype(jnp.bfloat16)
    values = proj[2].astype(jnp.bfloat16).reshape(rows_all, heads_local, HD)

    qkv = jnp.stack([queries[:prompt_rows], keys[:prompt_rows], values[:prompt_rows]], 0)
    qkv = qkv.reshape(3, seqs, pos_dev, heads_local, HD).transpose(1, 3, 0, 2, 4)
    qkv = qkv.reshape(pairs, 3, pos_dev, HD)
    got = lax.all_to_all(qkv, "seq", 0, 0, tiled=True)
    full = got.transpose(1, 0, 2, 3).reshape(3, full_len, HD)

    owner = seq_index
    own_prompt = owner // heads_local
    new_q = queries[prompt_rows:].reshape(pairs, HD)[owner]
    new_k = keys[prompt_rows:].reshape(pairs, HD)[owner]
    new_v = values[prompt_rows:].reshape(pairs, HD)[owner]
    prompt_out, new_out = attend_pair(
        full[0], full[1], full[2], new_q, new_k, new_v, lengths[own_prompt]
    )

    pad = 8
    back = jnp.concatenate(
        [prompt_out.reshape(n_seq, pos_dev, HD), jnp.broadcast_to(new_out, (n_seq, pad, HD))], 1
    )
    ret = lax.all_to_all(back, "seq", 0, 0, tiled=True)
    ret = ret.reshape(seqs, heads_local, pos_dev + pad, HD)
    attn_rows = ret[:, :, :pos_dev].transpose(0, 2, 1, 3).reshape(prompt_rows, width_local)
    attn_new = ret[:, :, pos_dev].reshape(seqs, width_local)
    attention = jnp.concatenate([attn_rows, attn_new], 0)

    part = jnp.dot(attention, w_out, preferred_element_type=jnp.float32)
    summed = lax.psum_scatter(
        part.astype(jnp.bfloat16), "tp", scatter_dimension=1, tiled=True
    ).astype(jnp.float32)
    square = lax.psum(jnp.sum(summed * summed, -1), "tp")
    out = (
        local_rows.astype(jnp.float32)
        + summed * lax.rsqrt(square[:, None] / full_width + norm_eps) * post_gain
    ).astype(jnp.bfloat16)
    return (
        out[:prompt_rows].reshape(seqs, pos_dev, width_local),
        out[prompt_rows:],
    )


def solution(mesh):
    in_specs = (
        P(None, "seq", "tp"),
        P(None, "tp"),
        P(None, None, "tp"),
        P("tp", None),
        P("tp"),
        P("tp"),
        P("tp"),
        P(),
    )
    out_specs = (P(None, "seq", "tp"), P(None, "tp"))
    return jax.shard_map(body, mesh=mesh, in_specs=in_specs, out_specs=out_specs, check_vma=False)
```

```python
import jax
import jax.numpy as jnp
from jax import lax
from jax.sharding import PartitionSpec as P

HD = 128


rope_base = 500000.0
norm_eps = 1e-06
masked_fill = -1e30


def rotate(values, position):
    half = values.shape[-1] // 2
    freq = rope_base ** (-(jnp.arange(half, dtype=jnp.float32) * 2.0) / values.shape[-1])
    angle = position.astype(jnp.float32)[..., None] * freq
    cosine = jnp.cos(angle)
    sine = jnp.sin(angle)
    lower = values[..., :half]
    upper = values[..., half:]
    return jnp.concatenate([lower * cosine - upper * sine, upper * cosine + lower * sine], -1)


def tp_links(width):
    size = 8
    cross = [(i, i ^ 1) for i in range(size)]
    up = [(i, (i + 2) % size) for i in range(size)]
    down = [(i, (i - 2) % size) for i in range(size)]
    t = lax.axis_index("tp")
    y, x = t // 2, t % 2
    other = 1 - x

    def block(dy, side):
        return ((y + dy) % 4) * 2 + side

    order = {
        "own": block(0, x), "ax": block(0, other), "aup": block(-1, x), "adn": block(1, x),
        "m1": block(1, other), "m2": block(-1, other), "m3": block(2, x), "m4": block(2, other),
    }
    return cross, up, down, order


def tp_gather(piece):
    width = piece.shape[1]
    half, quarter = width // 2, width // 4
    cross, up, down, order = tp_links(width)
    send = lambda value, perm: lax.ppermute(value, "tp", perm)
    ax = send(piece, cross)
    aup = send(piece, up)
    adn = send(piece, down)
    bx = send(jnp.concatenate([adn[:, :half], aup[:, :half]], 1), cross)
    bdn = send(jnp.concatenate([ax[:, half:], adn[:, :half]], 1), down)
    bup = send(jnp.concatenate([ax[:, half:], aup[:, half:]], 1), up)
    m1 = jnp.concatenate([bx[:, :half], bdn[:, :half]], 1)
    m2 = jnp.concatenate([bx[:, half:], bup[:, :half]], 1)
    m3 = jnp.concatenate([bdn[:, half:], bup[:, half:]], 1)
    cx = send(m3[:, :half], cross)
    cdn = send(m1[:, half:half + quarter], down)
    cup = send(m2[:, half + quarter:], up)
    m4 = jnp.concatenate([cx, cdn, cup], 1)
    blocks = {"own": piece, "ax": ax, "aup": aup, "adn": adn, "m1": m1, "m2": m2, "m3": m3, "m4": m4}
    whole = jnp.zeros((piece.shape[0], width * 8), piece.dtype)
    for name, value in blocks.items():
        whole = lax.dynamic_update_slice_in_dim(whole, value, order[name] * width, 1)
    return whole


def tp_reduce_scatter(part, width):
    half, quarter = width // 2, width // 4
    cross, up, down, order = tp_links(width)
    send = lambda value, perm: lax.ppermute(value.astype(jnp.bfloat16), "tp", perm).astype(jnp.float32)
    b = {name: lax.dynamic_slice_in_dim(part, index * width, width, 1) for name, index in order.items()}
    rx = send(b["m4"][:, :half], cross)
    rup = send(b["m4"][:, half:half + quarter], up)
    rdn = send(b["m4"][:, half + quarter:], down)
    m1, m2, m3 = b["m1"], b["m2"], b["m3"]
    m3 = jnp.concatenate([m3[:, :half] + rx, m3[:, half:]], 1)
    m1 = jnp.concatenate([m1[:, :half], m1[:, half:half + quarter] + rup, m1[:, half + quarter:]], 1)
    m2 = jnp.concatenate([m2[:, :half + quarter], m2[:, half + quarter:] + rdn], 1)
    rx = send(jnp.concatenate([m1[:, :half], m2[:, :half]], 1), cross)
    rup = send(jnp.concatenate([m1[:, half:], m3[:, :half]], 1), up)
    rdn = send(jnp.concatenate([m2[:, half:], m3[:, half:]], 1), down)
    ax = jnp.concatenate([b["ax"][:, :half], b["ax"][:, half:] + rup[:, :half] + rdn[:, :half]], 1)
    adn = jnp.concatenate([b["adn"][:, :half] + rx[:, :half] + rup[:, half:], b["adn"][:, half:]], 1)
    aup = jnp.concatenate([b["aup"][:, :half] + rx[:, half:], b["aup"][:, half:] + rdn[:, half:]], 1)
    return b["own"] + send(ax, cross) + send(adn, up) + send(aup, down)


def tp_sum(values):
    for bit in (1, 2, 4):
        values = jax.tree.map(
            lambda v, bit=bit: v + lax.ppermute(v, "tp", [(i, i ^ bit) for i in range(8)]), values
        )
    return values


def attend_pair(q_all, k_all, v_all, q_new, k_new, v_new, length):
    count = q_all.shape[0]
    scale = HD ** (-0.5)
    scores = jnp.dot(q_all, k_all.T, preferred_element_type=jnp.float32) * scale
    query_pos = jnp.arange(count, dtype=jnp.int32)[:, None]
    key_pos = jnp.arange(count, dtype=jnp.int32)[None, :]
    valid = (key_pos <= query_pos) & (key_pos < length)
    scores = jnp.where(valid, scores, masked_fill)
    top = jnp.max(scores, -1, keepdims=True)
    weights = jnp.where(valid, jnp.exp(scores - top), 0.0)
    total = jnp.sum(weights, -1, keepdims=True)
    prompt_out = (
        jnp.dot(weights.astype(jnp.bfloat16), v_all, preferred_element_type=jnp.float32) / total
    ).astype(jnp.bfloat16)
    new_scores = jnp.dot(k_all, q_new, preferred_element_type=jnp.float32) * scale
    live = jnp.arange(count, dtype=jnp.int32) < length
    new_scores = jnp.where(live, new_scores, masked_fill)
    self_score = jnp.dot(q_new, k_new, preferred_element_type=jnp.float32) * scale
    new_top = jnp.maximum(jnp.max(new_scores), self_score)
    new_weights = jnp.where(live, jnp.exp(new_scores - new_top), 0.0)
    own_weight = jnp.exp(self_score - new_top)
    new_total = jnp.sum(new_weights) + own_weight
    own_rounded = lax.optimization_barrier(own_weight.astype(jnp.bfloat16)).astype(jnp.float32)
    numer = jnp.dot(new_weights.astype(jnp.bfloat16), v_all, preferred_element_type=jnp.float32)
    numer = numer + own_rounded * v_new.astype(jnp.float32)
    return prompt_out, (numer / new_total).astype(jnp.bfloat16)


def body(tokens, new_tokens, w_qkv, w_out, q_gain, k_gain, post_gain, lengths):
    seqs, pos_dev, width_local = tokens.shape
    heads_local = width_local // HD
    full_width = w_qkv.shape[1]
    n_seq = lax.axis_size("seq")
    pairs = seqs * heads_local
    assert pairs == n_seq
    prompt_rows = seqs * pos_dev
    full_len = pos_dev * n_seq
    flat_rows = tokens.reshape(prompt_rows, width_local)
    local_rows = jnp.concatenate([flat_rows, new_tokens], 0)
    all_rows = tp_gather(local_rows)
    proj = jnp.einsum("tn,cnf->ctf", all_rows, w_qkv, preferred_element_type=jnp.float32)
    query_raw, key_raw = proj[0], proj[1]
    query_sq, key_sq = tp_sum((jnp.sum(query_raw * query_raw, -1), jnp.sum(key_raw * key_raw, -1)))

    def normed(values, square_sum, gain):
        return values * lax.rsqrt(square_sum[:, None] / full_width + norm_eps) * gain

    seq_index = lax.axis_index("seq")
    query_pos = seq_index * pos_dev + jnp.arange(pos_dev, dtype=jnp.int32)
    row_pos = jnp.concatenate([jnp.tile(query_pos, seqs), lengths.astype(jnp.int32)], 0)
    rows_all = prompt_rows + seqs
    queries = rotate(
        normed(query_raw, query_sq, q_gain).reshape(rows_all, heads_local, HD), row_pos[:, None]
    ).astype(jnp.bfloat16)
    keys = rotate(
        normed(key_raw, key_sq, k_gain).reshape(rows_all, heads_local, HD), row_pos[:, None]
    ).astype(jnp.bfloat16)
    values = proj[2].astype(jnp.bfloat16).reshape(rows_all, heads_local, HD)

    qkv = jnp.stack([queries[:prompt_rows], keys[:prompt_rows], values[:prompt_rows]], 0)
    qkv = qkv.reshape(3, seqs, pos_dev, heads_local, HD).transpose(1, 3, 0, 2, 4)
    qkv = qkv.reshape(pairs, 3, pos_dev, HD)
    got = lax.all_to_all(qkv, "seq", 0, 0, tiled=True)
    full = got.transpose(1, 0, 2, 3).reshape(3, full_len, HD)

    owner = seq_index
    own_prompt = owner // heads_local
    new_q = queries[prompt_rows:].reshape(pairs, HD)[owner]
    new_k = keys[prompt_rows:].reshape(pairs, HD)[owner]
    new_v = values[prompt_rows:].reshape(pairs, HD)[owner]
    prompt_out, new_out = attend_pair(
        full[0], full[1], full[2], new_q, new_k, new_v, lengths[own_prompt]
    )

    pad = 8
    back = jnp.concatenate(
        [prompt_out.reshape(n_seq, pos_dev, HD), jnp.broadcast_to(new_out, (n_seq, pad, HD))], 1
    )
    ret = lax.all_to_all(back, "seq", 0, 0, tiled=True)
    ret = ret.reshape(seqs, heads_local, pos_dev + pad, HD)
    attn_rows = ret[:, :, :pos_dev].transpose(0, 2, 1, 3).reshape(prompt_rows, width_local)
    attn_new = ret[:, :, pos_dev].reshape(seqs, width_local)
    attention = jnp.concatenate([attn_rows, attn_new], 0)

    part = jnp.dot(attention, w_out, preferred_element_type=jnp.float32)
    summed = tp_reduce_scatter(part, width_local)
    square = tp_sum(jnp.sum(summed * summed, -1))
    out = (
        local_rows.astype(jnp.float32)
        + summed * lax.rsqrt(square[:, None] / full_width + norm_eps) * post_gain
    ).astype(jnp.bfloat16)
    return (
        out[:prompt_rows].reshape(seqs, pos_dev, width_local),
        out[prompt_rows:],
    )


def solution(mesh):
    in_specs = (
        P(None, "seq", "tp"),
        P(None, "tp"),
        P(None, None, "tp"),
        P("tp", None),
        P("tp"),
        P("tp"),
        P("tp"),
        P(),
    )
    out_specs = (P(None, "seq", "tp"), P(None, "tp"))
    return jax.shard_map(body, mesh=mesh, in_specs=in_specs, out_specs=out_specs, check_vma=False)
```

```python
import jax
import jax.numpy as jnp
from jax import lax
from jax.sharding import PartitionSpec as P

HD = 128


rope_base = 500000.0
norm_eps = 1e-06
masked_fill = -1e30


def rotate(values, position):
    half = values.shape[-1] // 2
    freq = rope_base ** (-(jnp.arange(half, dtype=jnp.float32) * 2.0) / values.shape[-1])
    angle = position.astype(jnp.float32)[..., None] * freq
    cosine = jnp.cos(angle)
    sine = jnp.sin(angle)
    lower = values[..., :half]
    upper = values[..., half:]
    return jnp.concatenate([lower * cosine - upper * sine, upper * cosine + lower * sine], -1)


RELATIVE = ("own", "ax", "aup", "adn", "m1", "m2", "m3", "m4")


def tp_links(width):
    size = 8
    cross = [(i, i ^ 1) for i in range(size)]
    up = [(i, (i + 2) % size) for i in range(size)]
    down = [(i, (i - 2) % size) for i in range(size)]
    t = lax.axis_index("tp")
    y, x = t // 2, t % 2
    other = 1 - x

    def block(dy, side):
        return ((y + dy) % 4) * 2 + side

    order = {
        "own": block(0, x), "ax": block(0, other), "aup": block(-1, x), "adn": block(1, x),
        "m1": block(1, other), "m2": block(-1, other), "m3": block(2, x), "m4": block(2, other),
    }
    return cross, up, down, order


def tp_gather(piece):
    width = piece.shape[1]
    half, quarter = width // 2, width // 4
    cross, up, down, order = tp_links(width)
    send = lambda value, perm: lax.ppermute(value, "tp", perm)
    ax = send(piece, cross)
    aup = send(piece, up)
    adn = send(piece, down)
    bx = send(jnp.concatenate([adn[:, :half], aup[:, :half]], 1), cross)
    bdn = send(jnp.concatenate([ax[:, half:], adn[:, :half]], 1), down)
    bup = send(jnp.concatenate([ax[:, half:], aup[:, half:]], 1), up)
    m1 = jnp.concatenate([bx[:, :half], bdn[:, :half]], 1)
    m2 = jnp.concatenate([bx[:, half:], bup[:, :half]], 1)
    m3 = jnp.concatenate([bdn[:, half:], bup[:, half:]], 1)
    cx = send(m3[:, :half], cross)
    cdn = send(m1[:, half:half + quarter], down)
    cup = send(m2[:, half + quarter:], up)
    m4 = jnp.concatenate([cx, cdn, cup], 1)
    return [[piece, ax, aup, adn], [m1, m2, m3], [m4]], order


def tp_reduce_scatter(b, width):
    half, quarter = width // 2, width // 4
    cross, up, down, order = tp_links(width)
    send = lambda value, perm: lax.ppermute(value.astype(jnp.bfloat16), "tp", perm).astype(jnp.float32)
    rx = send(b["m4"][:, :half], cross)
    rup = send(b["m4"][:, half:half + quarter], up)
    rdn = send(b["m4"][:, half + quarter:], down)
    m1, m2, m3 = b["m1"], b["m2"], b["m3"]
    m3 = jnp.concatenate([m3[:, :half] + rx, m3[:, half:]], 1)
    m1 = jnp.concatenate([m1[:, :half], m1[:, half:half + quarter] + rup, m1[:, half + quarter:]], 1)
    m2 = jnp.concatenate([m2[:, :half + quarter], m2[:, half + quarter:] + rdn], 1)
    rx = send(jnp.concatenate([m1[:, :half], m2[:, :half]], 1), cross)
    rup = send(jnp.concatenate([m1[:, half:], m3[:, :half]], 1), up)
    rdn = send(jnp.concatenate([m2[:, half:], m3[:, half:]], 1), down)
    ax = jnp.concatenate([b["ax"][:, :half], b["ax"][:, half:] + rup[:, :half] + rdn[:, :half]], 1)
    adn = jnp.concatenate([b["adn"][:, :half] + rx[:, :half] + rup[:, half:], b["adn"][:, half:]], 1)
    aup = jnp.concatenate([b["aup"][:, :half] + rx[:, half:], b["aup"][:, half:] + rdn[:, half:]], 1)
    return b["own"] + send(ax, cross) + send(adn, up) + send(aup, down)


def tp_sum(values):
    for bit in (1, 2, 4):
        values = jax.tree.map(
            lambda v, bit=bit: v + lax.ppermute(v, "tp", [(i, i ^ bit) for i in range(8)]), values
        )
    return values


def attend_pair(q_all, k_all, v_all, q_new, k_new, v_new, length):
    count = q_all.shape[0]
    scale = HD ** (-0.5)
    chunks = 4
    size = count // chunks
    outs = []
    for c in range(chunks):
        stop = (c + 1) * size
        scores = (
            jnp.dot(q_all[c * size:stop], k_all[:stop].T, preferred_element_type=jnp.float32)
            * scale
        )
        query_pos = c * size + jnp.arange(size, dtype=jnp.int32)[:, None]
        key_pos = jnp.arange(stop, dtype=jnp.int32)[None, :]
        valid = (key_pos <= query_pos) & (key_pos < length)
        scores = jnp.where(valid, scores, masked_fill)
        top = jnp.max(scores, -1, keepdims=True)
        weights = jnp.where(valid, jnp.exp(scores - top), 0.0)
        total = jnp.sum(weights, -1, keepdims=True)
        outs.append(
            jnp.dot(weights.astype(jnp.bfloat16), v_all[:stop], preferred_element_type=jnp.float32)
            / total
        )
    prompt_out = jnp.concatenate(outs, 0).astype(jnp.bfloat16)
    new_scores = jnp.dot(k_all, q_new, preferred_element_type=jnp.float32) * scale
    live = jnp.arange(count, dtype=jnp.int32) < length
    new_scores = jnp.where(live, new_scores, masked_fill)
    self_score = jnp.dot(q_new, k_new, preferred_element_type=jnp.float32) * scale
    new_top = jnp.maximum(jnp.max(new_scores), self_score)
    new_weights = jnp.where(live, jnp.exp(new_scores - new_top), 0.0)
    own_weight = jnp.exp(self_score - new_top)
    new_total = jnp.sum(new_weights) + own_weight
    own_rounded = lax.optimization_barrier(own_weight.astype(jnp.bfloat16)).astype(jnp.float32)
    numer = jnp.dot(new_weights.astype(jnp.bfloat16), v_all, preferred_element_type=jnp.float32)
    numer = numer + own_rounded * v_new.astype(jnp.float32)
    return prompt_out, (numer / new_total).astype(jnp.bfloat16)


def body(tokens, new_tokens, w_qkv, w_out, q_gain, k_gain, post_gain, lengths):
    seqs, pos_dev, width_local = tokens.shape
    heads_local = width_local // HD
    full_width = w_qkv.shape[1]
    n_seq = lax.axis_size("seq")
    pairs = seqs * heads_local
    assert pairs == n_seq
    prompt_rows = seqs * pos_dev
    full_len = pos_dev * n_seq
    flat_rows = tokens.reshape(prompt_rows, width_local)
    local_rows = jnp.concatenate([flat_rows, new_tokens], 0)
    rounds, order = tp_gather(local_rows)

    def in_relative_order(weight, axis):
        return [
            lax.dynamic_slice_in_dim(weight, order[name] * width_local, width_local, axis)
            for name in RELATIVE
        ]

    w_blocks = in_relative_order(w_qkv, 1)
    proj, start = None, 0
    for blocks in rounds:
        stop = start + len(blocks)
        term = jnp.einsum(
            "tn,cnf->ctf",
            jnp.concatenate(blocks, 1),
            jnp.concatenate(w_blocks[start:stop], 1),
            preferred_element_type=jnp.float32,
        )
        proj = term if proj is None else proj + term
        start = stop
    query_raw, key_raw = proj[0], proj[1]
    query_sq, key_sq = tp_sum((jnp.sum(query_raw * query_raw, -1), jnp.sum(key_raw * key_raw, -1)))

    def normed(values, square_sum, gain):
        return values * lax.rsqrt(square_sum[:, None] / full_width + norm_eps) * gain

    seq_index = lax.axis_index("seq")
    query_pos = seq_index * pos_dev + jnp.arange(pos_dev, dtype=jnp.int32)
    row_pos = jnp.concatenate([jnp.tile(query_pos, seqs), lengths.astype(jnp.int32)], 0)
    rows_all = prompt_rows + seqs
    queries = rotate(
        normed(query_raw, query_sq, q_gain).reshape(rows_all, heads_local, HD), row_pos[:, None]
    ).astype(jnp.bfloat16)
    keys = rotate(
        normed(key_raw, key_sq, k_gain).reshape(rows_all, heads_local, HD), row_pos[:, None]
    ).astype(jnp.bfloat16)
    values = proj[2].astype(jnp.bfloat16).reshape(rows_all, heads_local, HD)

    qkv = jnp.stack([queries[:prompt_rows], keys[:prompt_rows], values[:prompt_rows]], 0)
    qkv = qkv.reshape(3, seqs, pos_dev, heads_local, HD).transpose(1, 3, 0, 2, 4)
    qkv = qkv.reshape(pairs, 3, pos_dev, HD)
    got = lax.all_to_all(qkv, "seq", 0, 0, tiled=True)
    full = got.transpose(1, 0, 2, 3).reshape(3, full_len, HD)

    owner = seq_index
    own_prompt = owner // heads_local
    new_q = queries[prompt_rows:].reshape(pairs, HD)[owner]
    new_k = keys[prompt_rows:].reshape(pairs, HD)[owner]
    new_v = values[prompt_rows:].reshape(pairs, HD)[owner]
    prompt_out, new_out = attend_pair(
        full[0], full[1], full[2], new_q, new_k, new_v, lengths[own_prompt]
    )

    pad = 8
    back = jnp.concatenate(
        [prompt_out.reshape(n_seq, pos_dev, HD), jnp.broadcast_to(new_out, (n_seq, pad, HD))], 1
    )
    ret = lax.all_to_all(back, "seq", 0, 0, tiled=True)
    ret = ret.reshape(seqs, heads_local, pos_dev + pad, HD)
    attn_rows = ret[:, :, :pos_dev].transpose(0, 2, 1, 3).reshape(prompt_rows, width_local)
    attn_new = ret[:, :, pos_dev].reshape(seqs, width_local)
    attention = jnp.concatenate([attn_rows, attn_new], 0)

    wo_blocks = in_relative_order(w_out, 1)
    part = {}
    for names in (RELATIVE[7:], RELATIVE[4:7], RELATIVE[:4]):
        columns = [wo_blocks[RELATIVE.index(name)] for name in names]
        value = jnp.dot(attention, jnp.concatenate(columns, 1), preferred_element_type=jnp.float32)
        for i, name in enumerate(names):
            part[name] = value[:, i * width_local:(i + 1) * width_local]
    summed = tp_reduce_scatter(part, width_local)
    square = tp_sum(jnp.sum(summed * summed, -1))
    out = (
        local_rows.astype(jnp.float32)
        + summed * lax.rsqrt(square[:, None] / full_width + norm_eps) * post_gain
    ).astype(jnp.bfloat16)
    return (
        out[:prompt_rows].reshape(seqs, pos_dev, width_local),
        out[prompt_rows:],
    )


def solution(mesh):
    in_specs = (
        P(None, "seq", "tp"),
        P(None, "tp"),
        P(None, None, "tp"),
        P("tp", None),
        P("tp"),
        P("tp"),
        P("tp"),
        P(),
    )
    out_specs = (P(None, "seq", "tp"), P(None, "tp"))
    return jax.shard_map(body, mesh=mesh, in_specs=in_specs, out_specs=out_specs, check_vma=False)
```

```python
import jax
import jax.numpy as jnp
from jax import lax
from jax.experimental import pallas as pl
from jax.experimental.pallas import tpu as pltpu
from jax.sharding import PartitionSpec as P

HD = 128


rope_base = 500000.0
norm_eps = 1e-06
masked_fill = -1e30


def rotate(values, position):
    half = values.shape[-1] // 2
    freq = rope_base ** (-(jnp.arange(half, dtype=jnp.float32) * 2.0) / values.shape[-1])
    angle = position.astype(jnp.float32)[..., None] * freq
    cosine = jnp.cos(angle)
    sine = jnp.sin(angle)
    lower = values[..., :half]
    upper = values[..., half:]
    return jnp.concatenate([lower * cosine - upper * sine, upper * cosine + lower * sine], -1)


RELATIVE = ("own", "ax", "aup", "adn", "m1", "m2", "m3", "m4")


def tp_links(width):
    size = 8
    cross = [(i, i ^ 1) for i in range(size)]
    up = [(i, (i + 2) % size) for i in range(size)]
    down = [(i, (i - 2) % size) for i in range(size)]
    t = lax.axis_index("tp")
    y, x = t // 2, t % 2
    other = 1 - x

    def block(dy, side):
        return ((y + dy) % 4) * 2 + side

    order = {
        "own": block(0, x), "ax": block(0, other), "aup": block(-1, x), "adn": block(1, x),
        "m1": block(1, other), "m2": block(-1, other), "m3": block(2, x), "m4": block(2, other),
    }
    return cross, up, down, order


def tp_gather(piece):
    width = piece.shape[1]
    half, quarter = width // 2, width // 4
    cross, up, down, order = tp_links(width)
    send = lambda value, perm: lax.ppermute(value, "tp", perm)
    ax = send(piece, cross)
    aup = send(piece, up)
    adn = send(piece, down)
    bx = send(jnp.concatenate([adn[:, :half], aup[:, :half]], 1), cross)
    bdn = send(jnp.concatenate([ax[:, half:], adn[:, :half]], 1), down)
    bup = send(jnp.concatenate([ax[:, half:], aup[:, half:]], 1), up)
    m1 = jnp.concatenate([bx[:, :half], bdn[:, :half]], 1)
    m2 = jnp.concatenate([bx[:, half:], bup[:, :half]], 1)
    m3 = jnp.concatenate([bdn[:, half:], bup[:, half:]], 1)
    cx = send(m3[:, :half], cross)
    cdn = send(m1[:, half:half + quarter], down)
    cup = send(m2[:, half + quarter:], up)
    m4 = jnp.concatenate([cx, cdn, cup], 1)
    return [[piece, ax, aup, adn], [m1, m2, m3], [m4]], order


def tp_reduce_scatter(b, width):
    half, quarter = width // 2, width // 4
    cross, up, down, order = tp_links(width)
    send = lambda value, perm: lax.ppermute(value.astype(jnp.bfloat16), "tp", perm).astype(jnp.float32)
    rx = send(b["m4"][:, :half], cross)
    rup = send(b["m4"][:, half:half + quarter], up)
    rdn = send(b["m4"][:, half + quarter:], down)
    m1, m2, m3 = b["m1"], b["m2"], b["m3"]
    m3 = jnp.concatenate([m3[:, :half] + rx, m3[:, half:]], 1)
    m1 = jnp.concatenate([m1[:, :half], m1[:, half:half + quarter] + rup, m1[:, half + quarter:]], 1)
    m2 = jnp.concatenate([m2[:, :half + quarter], m2[:, half + quarter:] + rdn], 1)
    rx = send(jnp.concatenate([m1[:, :half], m2[:, :half]], 1), cross)
    rup = send(jnp.concatenate([m1[:, half:], m3[:, :half]], 1), up)
    rdn = send(jnp.concatenate([m2[:, half:], m3[:, half:]], 1), down)
    ax = jnp.concatenate([b["ax"][:, :half], b["ax"][:, half:] + rup[:, :half] + rdn[:, :half]], 1)
    adn = jnp.concatenate([b["adn"][:, :half] + rx[:, :half] + rup[:, half:], b["adn"][:, half:]], 1)
    aup = jnp.concatenate([b["aup"][:, :half] + rx[:, half:], b["aup"][:, half:] + rdn[:, half:]], 1)
    return b["own"] + send(ax, cross) + send(adn, up) + send(aup, down)


def tp_sum(values):
    for bit in (1, 2, 4):
        values = jax.tree.map(
            lambda v, bit=bit: v + lax.ppermute(v, "tp", [(i, i ^ bit) for i in range(8)]), values
        )
    return values


def rope_pack(proj, square, gains, cosine, sine, seqs, pos_dev, full_width):
    _, rows, width = proj.shape
    heads = width // HD

    def kernel(proj_ref, square_ref, gain_ref, cos_ref, sin_ref, pack_ref, fresh_ref):
        cos_v = cos_ref[...]
        sin_v = sin_ref[...]
        for c in range(3):
            x = proj_ref[c]
            if c < 2:
                x = x * lax.rsqrt(square_ref[c] / full_width + norm_eps) * gain_ref[c]
            for h in range(heads):
                xh = x[:, h * HD:(h + 1) * HD]
                if c < 2:
                    xh = xh * cos_v + pltpu.roll(xh, HD // 2, 1) * sin_v
                xh = xh.astype(jnp.bfloat16)
                for b in range(seqs):
                    pack_ref[b * heads + h, c] = xh[b * pos_dev:(b + 1) * pos_dev]
                fresh_ref[c, :, h * HD:(h + 1) * HD] = xh[seqs * pos_dev:].astype(jnp.float32)

    return pl.pallas_call(
        kernel,
        out_shape=(
            jax.ShapeDtypeStruct((seqs * heads, 3, pos_dev, HD), jnp.bfloat16),
            jax.ShapeDtypeStruct((3, rows - seqs * pos_dev, width), jnp.float32),
        ),
    )(proj, square, gains, cosine, sine)


def attend_pair(q_all, k_all, v_all, q_new, k_new, v_new, length):
    count = q_all.shape[0]
    scale = HD ** (-0.5)
    chunks = 4
    size = count // chunks
    outs = []
    for c in range(chunks):
        stop = (c + 1) * size
        scores = (
            jnp.dot(q_all[c * size:stop], k_all[:stop].T, preferred_element_type=jnp.float32)
            * scale
        )
        query_pos = c * size + jnp.arange(size, dtype=jnp.int32)[:, None]
        key_pos = jnp.arange(stop, dtype=jnp.int32)[None, :]
        valid = (key_pos <= query_pos) & (key_pos < length)
        scores = jnp.where(valid, scores, masked_fill)
        top = jnp.max(scores, -1, keepdims=True)
        weights = jnp.where(valid, jnp.exp(scores - top), 0.0)
        total = jnp.sum(weights, -1, keepdims=True)
        outs.append(
            jnp.dot(weights.astype(jnp.bfloat16), v_all[:stop], preferred_element_type=jnp.float32)
            / total
        )
    prompt_out = jnp.concatenate(outs, 0).astype(jnp.bfloat16)
    new_scores = jnp.dot(k_all, q_new, preferred_element_type=jnp.float32) * scale
    live = jnp.arange(count, dtype=jnp.int32) < length
    new_scores = jnp.where(live, new_scores, masked_fill)
    self_score = jnp.dot(q_new, k_new, preferred_element_type=jnp.float32) * scale
    new_top = jnp.maximum(jnp.max(new_scores), self_score)
    new_weights = jnp.where(live, jnp.exp(new_scores - new_top), 0.0)
    own_weight = jnp.exp(self_score - new_top)
    new_total = jnp.sum(new_weights) + own_weight
    own_rounded = lax.optimization_barrier(own_weight.astype(jnp.bfloat16)).astype(jnp.float32)
    numer = jnp.dot(new_weights.astype(jnp.bfloat16), v_all, preferred_element_type=jnp.float32)
    numer = numer + own_rounded * v_new.astype(jnp.float32)
    return prompt_out, (numer / new_total).astype(jnp.bfloat16)


def body(tokens, new_tokens, w_qkv, w_out, q_gain, k_gain, post_gain, lengths):
    seqs, pos_dev, width_local = tokens.shape
    heads_local = width_local // HD
    full_width = w_qkv.shape[1]
    n_seq = lax.axis_size("seq")
    pairs = seqs * heads_local
    assert pairs == n_seq
    prompt_rows = seqs * pos_dev
    full_len = pos_dev * n_seq
    flat_rows = tokens.reshape(prompt_rows, width_local)
    local_rows = jnp.concatenate([flat_rows, new_tokens], 0)
    rounds, order = tp_gather(local_rows)

    def in_relative_order(weight, axis):
        return [
            lax.dynamic_slice_in_dim(weight, order[name] * width_local, width_local, axis)
            for name in RELATIVE
        ]

    w_blocks = in_relative_order(w_qkv, 1)
    proj, start = None, 0
    for blocks in rounds:
        stop = start + len(blocks)
        term = jnp.einsum(
            "tn,cnf->ctf",
            jnp.concatenate(blocks, 1),
            jnp.concatenate(w_blocks[start:stop], 1),
            preferred_element_type=jnp.float32,
        )
        proj = term if proj is None else proj + term
        start = stop
    query_raw, key_raw = proj[0], proj[1]
    query_sq, key_sq = tp_sum((jnp.sum(query_raw * query_raw, -1), jnp.sum(key_raw * key_raw, -1)))

    seq_index = lax.axis_index("seq")
    query_pos = seq_index * pos_dev + jnp.arange(pos_dev, dtype=jnp.int32)
    row_pos = jnp.concatenate([jnp.tile(query_pos, seqs), lengths.astype(jnp.int32)], 0)
    half = HD // 2
    freq = rope_base ** (-(jnp.arange(half, dtype=jnp.float32) * 2.0) / HD)
    angle = row_pos.astype(jnp.float32)[:, None] * freq
    cosine, sine = jnp.cos(angle), jnp.sin(angle)
    qkv, fresh = rope_pack(
        proj,
        jnp.stack([query_sq, key_sq])[:, :, None],
        jnp.stack([q_gain, k_gain])[:, None, :],
        jnp.concatenate([cosine, cosine], 1),
        jnp.concatenate([-sine, sine], 1),
        seqs,
        pos_dev,
        full_width,
    )

    got = lax.all_to_all(qkv, "seq", 0, 0, tiled=True)
    full = got.transpose(1, 0, 2, 3).reshape(3, full_len, HD)

    owner = seq_index
    own_prompt = owner // heads_local
    fresh = fresh.astype(jnp.bfloat16).reshape(3, pairs, HD)
    new_q, new_k, new_v = fresh[0, owner], fresh[1, owner], fresh[2, owner]
    prompt_out, new_out = attend_pair(
        full[0], full[1], full[2], new_q, new_k, new_v, lengths[own_prompt]
    )

    pad = 8
    back = jnp.concatenate(
        [prompt_out.reshape(n_seq, pos_dev, HD), jnp.broadcast_to(new_out, (n_seq, pad, HD))], 1
    )
    ret = lax.all_to_all(back, "seq", 0, 0, tiled=True)
    ret = ret.reshape(seqs, heads_local, pos_dev + pad, HD)
    attn_rows = ret[:, :, :pos_dev].transpose(0, 2, 1, 3).reshape(prompt_rows, width_local)
    attn_new = ret[:, :, pos_dev].reshape(seqs, width_local)
    attention = jnp.concatenate([attn_rows, attn_new], 0)

    wo_blocks = in_relative_order(w_out, 1)
    part = {}
    for names in (RELATIVE[7:], RELATIVE[4:7], RELATIVE[:4]):
        columns = [wo_blocks[RELATIVE.index(name)] for name in names]
        value = jnp.dot(attention, jnp.concatenate(columns, 1), preferred_element_type=jnp.float32)
        for i, name in enumerate(names):
            part[name] = value[:, i * width_local:(i + 1) * width_local]
    summed = tp_reduce_scatter(part, width_local)
    square = tp_sum(jnp.sum(summed * summed, -1))
    out = (
        local_rows.astype(jnp.float32)
        + summed * lax.rsqrt(square[:, None] / full_width + norm_eps) * post_gain
    ).astype(jnp.bfloat16)
    return (
        out[:prompt_rows].reshape(seqs, pos_dev, width_local),
        out[prompt_rows:],
    )


def solution(mesh):
    in_specs = (
        P(None, "seq", "tp"),
        P(None, "tp"),
        P(None, None, "tp"),
        P("tp", None),
        P("tp"),
        P("tp"),
        P("tp"),
        P(),
    )
    out_specs = (P(None, "seq", "tp"), P(None, "tp"))
    return jax.shard_map(body, mesh=mesh, in_specs=in_specs, out_specs=out_specs, check_vma=False)
```

```python
import jax
import jax.numpy as jnp
from jax import lax
from jax.experimental import pallas as pl
from jax.experimental.pallas import tpu as pltpu
from jax.sharding import PartitionSpec as P

HD = 128


rope_base = 500000.0
norm_eps = 1e-06
masked_fill = -1e30


def rotate(values, position):
    half = values.shape[-1] // 2
    freq = rope_base ** (-(jnp.arange(half, dtype=jnp.float32) * 2.0) / values.shape[-1])
    angle = position.astype(jnp.float32)[..., None] * freq
    cosine = jnp.cos(angle)
    sine = jnp.sin(angle)
    lower = values[..., :half]
    upper = values[..., half:]
    return jnp.concatenate([lower * cosine - upper * sine, upper * cosine + lower * sine], -1)


RELATIVE = ("own", "ax", "aup", "adn", "m1", "m2", "m3", "m4")


def tp_links(width):
    size = 8
    cross = [(i, i ^ 1) for i in range(size)]
    up = [(i, (i + 2) % size) for i in range(size)]
    down = [(i, (i - 2) % size) for i in range(size)]
    t = lax.axis_index("tp")
    y, x = t // 2, t % 2
    other = 1 - x

    def block(dy, side):
        return ((y + dy) % 4) * 2 + side

    order = {
        "own": block(0, x), "ax": block(0, other), "aup": block(-1, x), "adn": block(1, x),
        "m1": block(1, other), "m2": block(-1, other), "m3": block(2, x), "m4": block(2, other),
    }
    return cross, up, down, order


def tp_gather(piece):
    width = piece.shape[1]
    half, quarter = width // 2, width // 4
    cross, up, down, order = tp_links(width)
    send = lambda value, perm: lax.ppermute(value, "tp", perm)
    ax = send(piece, cross)
    aup = send(piece, up)
    adn = send(piece, down)
    bx = send(jnp.concatenate([adn[:, :half], aup[:, :half]], 1), cross)
    bdn = send(jnp.concatenate([ax[:, half:], adn[:, :half]], 1), down)
    bup = send(jnp.concatenate([ax[:, half:], aup[:, half:]], 1), up)
    m1 = jnp.concatenate([bx[:, :half], bdn[:, :half]], 1)
    m2 = jnp.concatenate([bx[:, half:], bup[:, :half]], 1)
    m3 = jnp.concatenate([bdn[:, half:], bup[:, half:]], 1)
    cx = send(m3[:, :half], cross)
    cdn = send(m1[:, half:half + quarter], down)
    cup = send(m2[:, half + quarter:], up)
    m4 = jnp.concatenate([cx, cdn, cup], 1)
    return [[piece, ax, aup, adn], [m1, m2, m3], [m4]], order


def tp_reduce_scatter(b, width):
    half, quarter = width // 2, width // 4
    cross, up, down, order = tp_links(width)
    send = lambda value, perm: lax.ppermute(value.astype(jnp.bfloat16), "tp", perm).astype(jnp.float32)
    rx = send(b["m4"][:, :half], cross)
    rup = send(b["m4"][:, half:half + quarter], up)
    rdn = send(b["m4"][:, half + quarter:], down)
    m1, m2, m3 = b["m1"], b["m2"], b["m3"]
    m3 = jnp.concatenate([m3[:, :half] + rx, m3[:, half:]], 1)
    m1 = jnp.concatenate([m1[:, :half], m1[:, half:half + quarter] + rup, m1[:, half + quarter:]], 1)
    m2 = jnp.concatenate([m2[:, :half + quarter], m2[:, half + quarter:] + rdn], 1)
    rx = send(jnp.concatenate([m1[:, :half], m2[:, :half]], 1), cross)
    rup = send(jnp.concatenate([m1[:, half:], m3[:, :half]], 1), up)
    rdn = send(jnp.concatenate([m2[:, half:], m3[:, half:]], 1), down)
    ax = jnp.concatenate([b["ax"][:, :half], b["ax"][:, half:] + rup[:, :half] + rdn[:, :half]], 1)
    adn = jnp.concatenate([b["adn"][:, :half] + rx[:, :half] + rup[:, half:], b["adn"][:, half:]], 1)
    aup = jnp.concatenate([b["aup"][:, :half] + rx[:, half:], b["aup"][:, half:] + rdn[:, half:]], 1)
    return b["own"] + send(ax, cross) + send(adn, up) + send(aup, down)


def tp_sum(values):
    for bit in (1, 2, 4):
        values = jax.tree.map(
            lambda v, bit=bit: v + lax.ppermute(v, "tp", [(i, i ^ bit) for i in range(8)]), values
        )
    return values


def rope_pack(proj, square, gains, cosine, sine, seqs, pos_dev, full_width):
    _, rows, width = proj.shape
    heads = width // HD

    def kernel(proj_ref, square_ref, gain_ref, cos_ref, sin_ref, pack_ref, fresh_ref):
        cos_v = cos_ref[...]
        sin_v = sin_ref[...]
        for c in range(3):
            x = proj_ref[c]
            if c < 2:
                x = x * lax.rsqrt(square_ref[c] / full_width + norm_eps) * gain_ref[c]
            for h in range(heads):
                xh = x[:, h * HD:(h + 1) * HD]
                if c < 2:
                    xh = xh * cos_v + pltpu.roll(xh, HD // 2, 1) * sin_v
                xh = xh.astype(jnp.bfloat16)
                for b in range(seqs):
                    pack_ref[b * heads + h, c] = xh[b * pos_dev:(b + 1) * pos_dev]
                fresh_ref[c, :, h * HD:(h + 1) * HD] = xh[seqs * pos_dev:].astype(jnp.float32)

    return pl.pallas_call(
        kernel,
        out_shape=(
            jax.ShapeDtypeStruct((seqs * heads, 3, pos_dev, HD), jnp.bfloat16),
            jax.ShapeDtypeStruct((3, rows - seqs * pos_dev, width), jnp.float32),
        ),
    )(proj, square, gains, cosine, sine)


def attend_pair(q_all, k_all, v_all, q_new, k_new, v_new, length):
    count = q_all.shape[0]
    scale = HD ** (-0.5)
    chunks = 2
    size = count // chunks
    outs = []
    for c in range(chunks):
        stop = (c + 1) * size
        scores = (
            jnp.dot(q_all[c * size:stop], k_all[:stop].T, preferred_element_type=jnp.float32)
            * scale
        )
        query_pos = c * size + jnp.arange(size, dtype=jnp.int32)[:, None]
        key_pos = jnp.arange(stop, dtype=jnp.int32)[None, :]
        valid = (key_pos <= query_pos) & (key_pos < length)
        scores = jnp.where(valid, scores, masked_fill)
        top = jnp.max(scores, -1, keepdims=True)
        weights = jnp.where(valid, jnp.exp(scores - top), 0.0)
        total = jnp.sum(weights, -1, keepdims=True)
        outs.append(
            jnp.dot(weights.astype(jnp.bfloat16), v_all[:stop], preferred_element_type=jnp.float32)
            / total
        )
    prompt_out = jnp.concatenate(outs, 0).astype(jnp.bfloat16)
    new_scores = jnp.dot(k_all, q_new, preferred_element_type=jnp.float32) * scale
    live = jnp.arange(count, dtype=jnp.int32) < length
    new_scores = jnp.where(live, new_scores, masked_fill)
    self_score = jnp.dot(q_new, k_new, preferred_element_type=jnp.float32) * scale
    new_top = jnp.maximum(jnp.max(new_scores), self_score)
    new_weights = jnp.where(live, jnp.exp(new_scores - new_top), 0.0)
    own_weight = jnp.exp(self_score - new_top)
    new_total = jnp.sum(new_weights) + own_weight
    own_rounded = lax.optimization_barrier(own_weight.astype(jnp.bfloat16)).astype(jnp.float32)
    numer = jnp.dot(new_weights.astype(jnp.bfloat16), v_all, preferred_element_type=jnp.float32)
    numer = numer + own_rounded * v_new.astype(jnp.float32)
    return prompt_out, (numer / new_total).astype(jnp.bfloat16)


def body(tokens, new_tokens, w_qkv, w_out, q_gain, k_gain, post_gain, lengths):
    seqs, pos_dev, width_local = tokens.shape
    heads_local = width_local // HD
    full_width = w_qkv.shape[1]
    n_seq = lax.axis_size("seq")
    pairs = seqs * heads_local
    assert pairs == n_seq
    prompt_rows = seqs * pos_dev
    full_len = pos_dev * n_seq
    flat_rows = tokens.reshape(prompt_rows, width_local)
    local_rows = jnp.concatenate([flat_rows, new_tokens], 0)
    rounds, order = tp_gather(local_rows)

    def in_relative_order(weight, axis):
        return [
            lax.dynamic_slice_in_dim(weight, order[name] * width_local, width_local, axis)
            for name in RELATIVE
        ]

    w_blocks = in_relative_order(w_qkv, 1)
    proj, start = None, 0
    for blocks in rounds:
        stop = start + len(blocks)
        term = jnp.einsum(
            "tn,cnf->ctf",
            jnp.concatenate(blocks, 1),
            jnp.concatenate(w_blocks[start:stop], 1),
            preferred_element_type=jnp.float32,
        )
        proj = term if proj is None else proj + term
        start = stop
    query_raw, key_raw = proj[0], proj[1]
    query_sq, key_sq = tp_sum((jnp.sum(query_raw * query_raw, -1), jnp.sum(key_raw * key_raw, -1)))

    seq_index = lax.axis_index("seq")
    query_pos = seq_index * pos_dev + jnp.arange(pos_dev, dtype=jnp.int32)
    row_pos = jnp.concatenate([jnp.tile(query_pos, seqs), lengths.astype(jnp.int32)], 0)
    half = HD // 2
    freq = rope_base ** (-(jnp.arange(half, dtype=jnp.float32) * 2.0) / HD)
    angle = row_pos.astype(jnp.float32)[:, None] * freq
    cosine, sine = jnp.cos(angle), jnp.sin(angle)
    qkv, fresh = rope_pack(
        proj,
        jnp.stack([query_sq, key_sq])[:, :, None],
        jnp.stack([q_gain, k_gain])[:, None, :],
        jnp.concatenate([cosine, cosine], 1),
        jnp.concatenate([-sine, sine], 1),
        seqs,
        pos_dev,
        full_width,
    )

    got = lax.all_to_all(qkv, "seq", 0, 0, tiled=True)
    full = got.transpose(1, 0, 2, 3).reshape(3, full_len, HD)

    owner = seq_index
    own_prompt = owner // heads_local
    fresh = fresh.astype(jnp.bfloat16).reshape(3, pairs, HD)
    new_q, new_k, new_v = fresh[0, owner], fresh[1, owner], fresh[2, owner]
    prompt_out, new_out = attend_pair(
        full[0], full[1], full[2], new_q, new_k, new_v, lengths[own_prompt]
    )

    pad = 8
    back = jnp.concatenate(
        [prompt_out.reshape(n_seq, pos_dev, HD), jnp.broadcast_to(new_out, (n_seq, pad, HD))], 1
    )
    ret = lax.all_to_all(back, "seq", 0, 0, tiled=True)
    ret = ret.reshape(seqs, heads_local, pos_dev + pad, HD)
    attn_rows = ret[:, :, :pos_dev].transpose(0, 2, 1, 3).reshape(prompt_rows, width_local)
    attn_new = ret[:, :, pos_dev].reshape(seqs, width_local)
    attention = jnp.concatenate([attn_rows, attn_new], 0)

    wo_blocks = in_relative_order(w_out, 1)
    part = {}
    for names in (RELATIVE[7:], RELATIVE[4:7], RELATIVE[:4]):
        columns = [wo_blocks[RELATIVE.index(name)] for name in names]
        value = jnp.dot(attention, jnp.concatenate(columns, 1), preferred_element_type=jnp.float32)
        for i, name in enumerate(names):
            part[name] = value[:, i * width_local:(i + 1) * width_local]
    summed = tp_reduce_scatter(part, width_local)
    square = tp_sum(jnp.sum(summed * summed, -1))
    out = (
        local_rows.astype(jnp.float32)
        + summed * lax.rsqrt(square[:, None] / full_width + norm_eps) * post_gain
    ).astype(jnp.bfloat16)
    return (
        out[:prompt_rows].reshape(seqs, pos_dev, width_local),
        out[prompt_rows:],
    )


def solution(mesh):
    in_specs = (
        P(None, "seq", "tp"),
        P(None, "tp"),
        P(None, None, "tp"),
        P("tp", None),
        P("tp"),
        P("tp"),
        P("tp"),
        P(),
    )
    out_specs = (P(None, "seq", "tp"), P(None, "tp"))
    return jax.shard_map(body, mesh=mesh, in_specs=in_specs, out_specs=out_specs, check_vma=False)
```

```python
import jax
import jax.numpy as jnp
from jax import lax
from jax.experimental import pallas as pl
from jax.experimental.pallas import tpu as pltpu
from jax.sharding import PartitionSpec as P

HD = 128


rope_base = 500000.0
norm_eps = 1e-06
masked_fill = -1e30


RELATIVE = ("own", "ax", "aup", "adn", "m1", "m2", "m3", "m4")


def tp_links(width):
    size = 8
    cross = [(i, i ^ 1) for i in range(size)]
    up = [(i, (i + 2) % size) for i in range(size)]
    down = [(i, (i - 2) % size) for i in range(size)]
    t = lax.axis_index("tp")
    y, x = t // 2, t % 2
    other = 1 - x

    def block(dy, side):
        return ((y + dy) % 4) * 2 + side

    order = {
        "own": block(0, x), "ax": block(0, other), "aup": block(-1, x), "adn": block(1, x),
        "m1": block(1, other), "m2": block(-1, other), "m3": block(2, x), "m4": block(2, other),
    }
    return cross, up, down, order


def tp_gather(piece):
    width = piece.shape[1]
    half, quarter = width // 2, width // 4
    cross, up, down, order = tp_links(width)
    send = lambda value, perm: lax.ppermute(value, "tp", perm)
    ax = send(piece, cross)
    aup = send(piece, up)
    adn = send(piece, down)
    bx = send(jnp.concatenate([adn[:, :half], aup[:, :half]], 1), cross)
    bdn = send(jnp.concatenate([ax[:, half:], adn[:, :half]], 1), down)
    bup = send(jnp.concatenate([ax[:, half:], aup[:, half:]], 1), up)
    m1 = jnp.concatenate([bx[:, :half], bdn[:, :half]], 1)
    m2 = jnp.concatenate([bx[:, half:], bup[:, :half]], 1)
    m3 = jnp.concatenate([bdn[:, half:], bup[:, half:]], 1)
    cx = send(m3[:, :half], cross)
    cdn = send(m1[:, half:half + quarter], down)
    cup = send(m2[:, half + quarter:], up)
    m4 = jnp.concatenate([cx, cdn, cup], 1)
    return [[piece, ax, aup, adn], [m1, m2, m3], [m4]], order


def tp_reduce_scatter(b, width):
    half, quarter = width // 2, width // 4
    cross, up, down, order = tp_links(width)
    send = lambda value, perm: lax.ppermute(value.astype(jnp.bfloat16), "tp", perm).astype(jnp.float32)
    rx = send(b["m4"][:, :half], cross)
    rup = send(b["m4"][:, half:half + quarter], up)
    rdn = send(b["m4"][:, half + quarter:], down)
    m1, m2, m3 = b["m1"], b["m2"], b["m3"]
    m3 = jnp.concatenate([m3[:, :half] + rx, m3[:, half:]], 1)
    m1 = jnp.concatenate([m1[:, :half], m1[:, half:half + quarter] + rup, m1[:, half + quarter:]], 1)
    m2 = jnp.concatenate([m2[:, :half + quarter], m2[:, half + quarter:] + rdn], 1)
    rx = send(jnp.concatenate([m1[:, :half], m2[:, :half]], 1), cross)
    rup = send(jnp.concatenate([m1[:, half:], m3[:, :half]], 1), up)
    rdn = send(jnp.concatenate([m2[:, half:], m3[:, half:]], 1), down)
    ax = jnp.concatenate([b["ax"][:, :half], b["ax"][:, half:] + rup[:, :half] + rdn[:, :half]], 1)
    adn = jnp.concatenate([b["adn"][:, :half] + rx[:, :half] + rup[:, half:], b["adn"][:, half:]], 1)
    aup = jnp.concatenate([b["aup"][:, :half] + rx[:, half:], b["aup"][:, half:] + rdn[:, half:]], 1)
    return b["own"] + send(ax, cross) + send(adn, up) + send(aup, down)


def tp_sum(values):
    for bit in (1, 2, 4):
        values = jax.tree.map(
            lambda v, bit=bit: v + lax.ppermute(v, "tp", [(i, i ^ bit) for i in range(8)]), values
        )
    return values


def rope_pack(proj, square, gains, cosine, sine, seqs, pos_dev, full_width):
    _, rows, width = proj.shape
    heads = width // HD

    def kernel(proj_ref, square_ref, gain_ref, cos_ref, sin_ref, pack_ref, fresh_ref):
        cos_v = cos_ref[...]
        sin_v = sin_ref[...]
        for c in range(3):
            x = proj_ref[c]
            if c < 2:
                x = x * lax.rsqrt(square_ref[c] / full_width + norm_eps) * gain_ref[c]
            for h in range(heads):
                xh = x[:, h * HD:(h + 1) * HD]
                if c < 2:
                    xh = xh * cos_v + pltpu.roll(xh, HD // 2, 1) * sin_v
                xh = xh.astype(jnp.bfloat16)
                for b in range(seqs):
                    pack_ref[b * heads + h, c] = xh[b * pos_dev:(b + 1) * pos_dev]
                fresh_ref[c, :, h * HD:(h + 1) * HD] = xh[seqs * pos_dev:].astype(jnp.float32)

    return pl.pallas_call(
        kernel,
        out_shape=(
            jax.ShapeDtypeStruct((seqs * heads, 3, pos_dev, HD), jnp.bfloat16),
            jax.ShapeDtypeStruct((3, rows - seqs * pos_dev, width), jnp.float32),
        ),
    )(proj, square, gains, cosine, sine)


def attend_pair(q_all, k_all, v_all, q_new, k_new, v_new, length):
    count = q_all.shape[0]
    scale = HD ** (-0.5)
    chunks = 2
    size = count // chunks
    outs = []
    for c in range(chunks):
        stop = (c + 1) * size
        scores = (
            jnp.dot(q_all[c * size:stop], k_all[:stop].T, preferred_element_type=jnp.float32)
            * scale
        )
        query_pos = c * size + jnp.arange(size, dtype=jnp.int32)[:, None]
        key_pos = jnp.arange(stop, dtype=jnp.int32)[None, :]
        valid = (key_pos <= query_pos) & (key_pos < length)
        scores = jnp.where(valid, scores, masked_fill)
        top = jnp.max(scores, -1, keepdims=True)
        weights = jnp.where(valid, jnp.exp(scores - top), 0.0)
        total = jnp.sum(weights, -1, keepdims=True)
        outs.append(
            jnp.dot(weights.astype(jnp.bfloat16), v_all[:stop], preferred_element_type=jnp.float32)
            / total
        )
    prompt_out = jnp.concatenate(outs, 0).astype(jnp.bfloat16)
    new_scores = jnp.dot(k_all, q_new, preferred_element_type=jnp.float32) * scale
    live = jnp.arange(count, dtype=jnp.int32) < length
    new_scores = jnp.where(live, new_scores, masked_fill)
    self_score = jnp.dot(q_new, k_new, preferred_element_type=jnp.float32) * scale
    new_top = jnp.maximum(jnp.max(new_scores), self_score)
    new_weights = jnp.where(live, jnp.exp(new_scores - new_top), 0.0)
    own_weight = jnp.exp(self_score - new_top)
    new_total = jnp.sum(new_weights) + own_weight
    own_rounded = lax.optimization_barrier(own_weight.astype(jnp.bfloat16)).astype(jnp.float32)
    numer = jnp.dot(new_weights.astype(jnp.bfloat16), v_all, preferred_element_type=jnp.float32)
    numer = numer + own_rounded * v_new.astype(jnp.float32)
    return prompt_out, (numer / new_total).astype(jnp.bfloat16)


def body(tokens, new_tokens, w_qkv, w_out, q_gain, k_gain, post_gain, lengths):
    seqs, pos_dev, width_local = tokens.shape
    heads_local = width_local // HD
    full_width = w_qkv.shape[1]
    n_seq = lax.axis_size("seq")
    pairs = seqs * heads_local
    assert pairs == n_seq
    prompt_rows = seqs * pos_dev
    full_len = pos_dev * n_seq
    flat_rows = tokens.reshape(prompt_rows, width_local)
    local_rows = jnp.concatenate([flat_rows, new_tokens], 0)
    rounds, order = tp_gather(local_rows)

    def in_relative_order(weight, axis):
        return [
            lax.dynamic_slice_in_dim(weight, order[name] * width_local, width_local, axis)
            for name in RELATIVE
        ]

    w_blocks = in_relative_order(w_qkv, 1)
    proj, start = None, 0
    for blocks in rounds:
        stop = start + len(blocks)
        term = jnp.einsum(
            "tn,cnf->ctf",
            jnp.concatenate(blocks, 1),
            jnp.concatenate(w_blocks[start:stop], 1),
            preferred_element_type=jnp.float32,
        )
        proj = term if proj is None else proj + term
        start = stop
    query_raw, key_raw = proj[0], proj[1]
    squares = tp_sum(jnp.stack([jnp.sum(query_raw * query_raw, -1), jnp.sum(key_raw * key_raw, -1)]))

    seq_index = lax.axis_index("seq")
    query_pos = seq_index * pos_dev + jnp.arange(pos_dev, dtype=jnp.int32)
    row_pos = jnp.concatenate([jnp.tile(query_pos, seqs), lengths.astype(jnp.int32)], 0)
    half = HD // 2
    freq = rope_base ** (-(jnp.arange(half, dtype=jnp.float32) * 2.0) / HD)
    angle = row_pos.astype(jnp.float32)[:, None] * freq
    cosine, sine = jnp.cos(angle), jnp.sin(angle)
    qkv, fresh = rope_pack(
        proj,
        squares[:, :, None],
        jnp.stack([q_gain, k_gain])[:, None, :],
        jnp.concatenate([cosine, cosine], 1),
        jnp.concatenate([-sine, sine], 1),
        seqs,
        pos_dev,
        full_width,
    )

    got = lax.all_to_all(qkv, "seq", 0, 0, tiled=True)
    full = got.transpose(1, 0, 2, 3).reshape(3, full_len, HD)

    owner = seq_index
    own_prompt = owner // heads_local
    fresh = fresh.astype(jnp.bfloat16).reshape(3, pairs, HD)
    new_q, new_k, new_v = fresh[0, owner], fresh[1, owner], fresh[2, owner]
    prompt_out, new_out = attend_pair(
        full[0], full[1], full[2], new_q, new_k, new_v, lengths[own_prompt]
    )

    pad = 8
    back = jnp.concatenate(
        [prompt_out.reshape(n_seq, pos_dev, HD), jnp.broadcast_to(new_out, (n_seq, pad, HD))], 1
    )
    ret = lax.all_to_all(back, "seq", 0, 0, tiled=True)
    ret = ret.reshape(seqs, heads_local, pos_dev + pad, HD)
    attn_rows = ret[:, :, :pos_dev].transpose(0, 2, 1, 3).reshape(prompt_rows, width_local)
    attn_new = ret[:, :, pos_dev].reshape(seqs, width_local)
    attention = jnp.concatenate([attn_rows, attn_new], 0)

    wo_blocks = in_relative_order(w_out, 1)
    part = {}
    for names in (RELATIVE[7:], RELATIVE[4:7], RELATIVE[:4]):
        columns = [wo_blocks[RELATIVE.index(name)] for name in names]
        value = jnp.dot(attention, jnp.concatenate(columns, 1), preferred_element_type=jnp.float32)
        for i, name in enumerate(names):
            part[name] = value[:, i * width_local:(i + 1) * width_local]
    summed = tp_reduce_scatter(part, width_local)
    square = tp_sum(jnp.sum(summed * summed, -1))
    out = (
        local_rows.astype(jnp.float32)
        + summed * lax.rsqrt(square[:, None] / full_width + norm_eps) * post_gain
    ).astype(jnp.bfloat16)
    return (
        out[:prompt_rows].reshape(seqs, pos_dev, width_local),
        out[prompt_rows:],
    )


def solution(mesh):
    in_specs = (
        P(None, "seq", "tp"),
        P(None, "tp"),
        P(None, None, "tp"),
        P("tp", None),
        P("tp"),
        P("tp"),
        P("tp"),
        P(),
    )
    out_specs = (P(None, "seq", "tp"), P(None, "tp"))
    return jax.shard_map(body, mesh=mesh, in_specs=in_specs, out_specs=out_specs, check_vma=False)
```

```python
import jax
import jax.numpy as jnp
from jax import lax
from jax.experimental import pallas as pl
from jax.experimental.pallas import tpu as pltpu
from jax.sharding import PartitionSpec as P

HD = 128


rope_base = 500000.0
norm_eps = 1e-06
masked_fill = -1e30


RELATIVE = ("own", "ax", "aup", "adn", "m1", "m2", "m3", "m4")


def tp_links(width):
    size = 8
    cross = [(i, i ^ 1) for i in range(size)]
    up = [(i, (i + 2) % size) for i in range(size)]
    down = [(i, (i - 2) % size) for i in range(size)]
    t = lax.axis_index("tp")
    y, x = t // 2, t % 2
    other = 1 - x

    def block(dy, side):
        return ((y + dy) % 4) * 2 + side

    order = {
        "own": block(0, x), "ax": block(0, other), "aup": block(-1, x), "adn": block(1, x),
        "m1": block(1, other), "m2": block(-1, other), "m3": block(2, x), "m4": block(2, other),
    }
    return cross, up, down, order


def tp_gather(piece):
    width = piece.shape[1]
    half, quarter = width // 2, width // 4
    cross, up, down, order = tp_links(width)
    send = lambda value, perm: lax.ppermute(value, "tp", perm)
    ax = send(piece, cross)
    aup = send(piece, up)
    adn = send(piece, down)
    bx = send(jnp.concatenate([adn[:, :half], aup[:, :half]], 1), cross)
    bdn = send(jnp.concatenate([ax[:, half:], adn[:, :half]], 1), down)
    bup = send(jnp.concatenate([ax[:, half:], aup[:, half:]], 1), up)
    m1 = jnp.concatenate([bx[:, :half], bdn[:, :half]], 1)
    m2 = jnp.concatenate([bx[:, half:], bup[:, :half]], 1)
    m3 = jnp.concatenate([bdn[:, half:], bup[:, half:]], 1)
    cx = send(m3[:, :half], cross)
    cdn = send(m1[:, half:half + quarter], down)
    cup = send(m2[:, half + quarter:], up)
    m4 = jnp.concatenate([cx, cdn, cup], 1)
    return [[piece, ax, aup, adn], [m1, m2, m3], [m4]], order


def tp_reduce_scatter(b, width):
    half, quarter = width // 2, width // 4
    cross, up, down, order = tp_links(width)
    send = lambda value, perm: lax.ppermute(value.astype(jnp.bfloat16), "tp", perm).astype(jnp.float32)
    rx = send(b["m4"][:, :half], cross)
    rup = send(b["m4"][:, half:half + quarter], up)
    rdn = send(b["m4"][:, half + quarter:], down)
    m1, m2, m3 = b["m1"], b["m2"], b["m3"]
    m3 = jnp.concatenate([m3[:, :half] + rx, m3[:, half:]], 1)
    m1 = jnp.concatenate([m1[:, :half], m1[:, half:half + quarter] + rup, m1[:, half + quarter:]], 1)
    m2 = jnp.concatenate([m2[:, :half + quarter], m2[:, half + quarter:] + rdn], 1)
    rx = send(jnp.concatenate([m1[:, :half], m2[:, :half]], 1), cross)
    rup = send(jnp.concatenate([m1[:, half:], m3[:, :half]], 1), up)
    rdn = send(jnp.concatenate([m2[:, half:], m3[:, half:]], 1), down)
    ax = jnp.concatenate([b["ax"][:, :half], b["ax"][:, half:] + rup[:, :half] + rdn[:, :half]], 1)
    adn = jnp.concatenate([b["adn"][:, :half] + rx[:, :half] + rup[:, half:], b["adn"][:, half:]], 1)
    aup = jnp.concatenate([b["aup"][:, :half] + rx[:, half:], b["aup"][:, half:] + rdn[:, half:]], 1)
    return b["own"] + send(ax, cross) + send(adn, up) + send(aup, down)


def tp_sum(values):
    for bit in (1, 2, 4):
        values = jax.tree.map(
            lambda v, bit=bit: v + lax.ppermute(v, "tp", [(i, i ^ bit) for i in range(8)]), values
        )
    return values


def rope_pack(proj, square, gains, cosine, sine, seqs, pos_dev, full_width):
    _, rows, width = proj.shape
    heads = width // HD

    def kernel(proj_ref, square_ref, gain_ref, cos_ref, sin_ref, pack_ref, fresh_ref):
        cos_v = cos_ref[...]
        sin_v = sin_ref[...]
        for c in range(3):
            x = proj_ref[c]
            if c < 2:
                x = x * lax.rsqrt(square_ref[c] / full_width + norm_eps) * gain_ref[c]
            for h in range(heads):
                xh = x[:, h * HD:(h + 1) * HD]
                if c < 2:
                    xh = xh * cos_v + pltpu.roll(xh, HD // 2, 1) * sin_v
                xh = xh.astype(jnp.bfloat16)
                for b in range(seqs):
                    pack_ref[b * heads + h, c] = xh[b * pos_dev:(b + 1) * pos_dev]
                fresh_ref[c, :, h * HD:(h + 1) * HD] = xh[seqs * pos_dev:].astype(jnp.float32)

    return pl.pallas_call(
        kernel,
        out_shape=(
            jax.ShapeDtypeStruct((seqs * heads, 3, pos_dev, HD), jnp.bfloat16),
            jax.ShapeDtypeStruct((3, rows - seqs * pos_dev, width), jnp.float32),
        ),
    )(proj, square, gains, cosine, sine)


def attend_pair(q_all, k_all, v_all, q_new, k_new, v_new, length):
    count = q_all.shape[0]
    scale = HD ** (-0.5)
    bounds = (0, count // 4, count // 2, count * 3 // 4, count)
    outs = []
    for begin, stop in zip(bounds[:-1], bounds[1:]):
        scores = (
            jnp.dot(q_all[begin:stop], k_all[:stop].T, preferred_element_type=jnp.float32)
            * scale
        )
        query_pos = begin + jnp.arange(stop - begin, dtype=jnp.int32)[:, None]
        key_pos = jnp.arange(stop, dtype=jnp.int32)[None, :]
        valid = (key_pos <= query_pos) & (key_pos < length)
        scores = jnp.where(valid, scores, masked_fill)
        top = jnp.max(scores, -1, keepdims=True)
        weights = jnp.where(valid, jnp.exp(scores - top), 0.0)
        total = jnp.sum(weights, -1, keepdims=True)
        outs.append(
            jnp.dot(weights.astype(jnp.bfloat16), v_all[:stop], preferred_element_type=jnp.float32)
            / total
        )
    prompt_out = jnp.concatenate(outs, 0).astype(jnp.bfloat16)
    new_scores = jnp.dot(k_all, q_new, preferred_element_type=jnp.float32) * scale
    live = jnp.arange(count, dtype=jnp.int32) < length
    new_scores = jnp.where(live, new_scores, masked_fill)
    self_score = jnp.dot(q_new, k_new, preferred_element_type=jnp.float32) * scale
    new_top = jnp.maximum(jnp.max(new_scores), self_score)
    new_weights = jnp.where(live, jnp.exp(new_scores - new_top), 0.0)
    own_weight = jnp.exp(self_score - new_top)
    new_total = jnp.sum(new_weights) + own_weight
    own_rounded = lax.optimization_barrier(own_weight.astype(jnp.bfloat16)).astype(jnp.float32)
    numer = jnp.dot(new_weights.astype(jnp.bfloat16), v_all, preferred_element_type=jnp.float32)
    numer = numer + own_rounded * v_new.astype(jnp.float32)
    return prompt_out, (numer / new_total).astype(jnp.bfloat16)


def body(tokens, new_tokens, w_qkv, w_out, q_gain, k_gain, post_gain, lengths):
    seqs, pos_dev, width_local = tokens.shape
    heads_local = width_local // HD
    full_width = w_qkv.shape[1]
    n_seq = lax.axis_size("seq")
    pairs = seqs * heads_local
    assert pairs == n_seq
    prompt_rows = seqs * pos_dev
    full_len = pos_dev * n_seq
    flat_rows = tokens.reshape(prompt_rows, width_local)
    local_rows = jnp.concatenate([flat_rows, new_tokens], 0)
    rounds, order = tp_gather(local_rows)

    def in_relative_order(weight, axis):
        return [
            lax.dynamic_slice_in_dim(weight, order[name] * width_local, width_local, axis)
            for name in RELATIVE
        ]

    w_blocks = in_relative_order(w_qkv, 1)
    proj, start = None, 0
    for blocks in rounds:
        stop = start + len(blocks)
        term = jnp.einsum(
            "tn,cnf->ctf",
            jnp.concatenate(blocks, 1),
            jnp.concatenate(w_blocks[start:stop], 1),
            preferred_element_type=jnp.float32,
        )
        proj = term if proj is None else proj + term
        start = stop
    query_raw, key_raw = proj[0], proj[1]
    squares = tp_sum(jnp.stack([jnp.sum(query_raw * query_raw, -1), jnp.sum(key_raw * key_raw, -1)]))

    seq_index = lax.axis_index("seq")
    query_pos = seq_index * pos_dev + jnp.arange(pos_dev, dtype=jnp.int32)
    row_pos = jnp.concatenate([jnp.tile(query_pos, seqs), lengths.astype(jnp.int32)], 0)
    half = HD // 2
    freq = rope_base ** (-(jnp.arange(half, dtype=jnp.float32) * 2.0) / HD)
    angle = row_pos.astype(jnp.float32)[:, None] * freq
    cosine, sine = jnp.cos(angle), jnp.sin(angle)
    qkv, fresh = rope_pack(
        proj,
        squares[:, :, None],
        jnp.stack([q_gain, k_gain])[:, None, :],
        jnp.concatenate([cosine, cosine], 1),
        jnp.concatenate([-sine, sine], 1),
        seqs,
        pos_dev,
        full_width,
    )

    got = lax.all_to_all(qkv, "seq", 0, 0, tiled=True)
    full = got.transpose(1, 0, 2, 3).reshape(3, full_len, HD)

    owner = seq_index
    own_prompt = owner // heads_local
    fresh = fresh.astype(jnp.bfloat16).reshape(3, pairs, HD)
    new_q, new_k, new_v = fresh[0, owner], fresh[1, owner], fresh[2, owner]
    prompt_out, new_out = attend_pair(
        full[0], full[1], full[2], new_q, new_k, new_v, lengths[own_prompt]
    )

    pad = 8
    back = jnp.concatenate(
        [prompt_out.reshape(n_seq, pos_dev, HD), jnp.broadcast_to(new_out, (n_seq, pad, HD))], 1
    )
    ret = lax.all_to_all(back, "seq", 0, 0, tiled=True)
    ret = ret.reshape(seqs, heads_local, pos_dev + pad, HD)
    attn_rows = ret[:, :, :pos_dev].transpose(0, 2, 1, 3).reshape(prompt_rows, width_local)
    attn_new = ret[:, :, pos_dev].reshape(seqs, width_local)
    attention = jnp.concatenate([attn_rows, attn_new], 0)

    wo_blocks = in_relative_order(w_out, 1)
    part = {}
    for names in (RELATIVE[7:], RELATIVE[4:7], RELATIVE[:4]):
        columns = [wo_blocks[RELATIVE.index(name)] for name in names]
        value = jnp.dot(attention, jnp.concatenate(columns, 1), preferred_element_type=jnp.float32)
        for i, name in enumerate(names):
            part[name] = value[:, i * width_local:(i + 1) * width_local]
    summed = tp_reduce_scatter(part, width_local)
    square = tp_sum(jnp.sum(summed * summed, -1))
    out = (
        local_rows.astype(jnp.float32)
        + summed * lax.rsqrt(square[:, None] / full_width + norm_eps) * post_gain
    ).astype(jnp.bfloat16)
    return (
        out[:prompt_rows].reshape(seqs, pos_dev, width_local),
        out[prompt_rows:],
    )


def solution(mesh):
    in_specs = (
        P(None, "seq", "tp"),
        P(None, "tp"),
        P(None, None, "tp"),
        P("tp", None),
        P("tp"),
        P("tp"),
        P("tp"),
        P(),
    )
    out_specs = (P(None, "seq", "tp"), P(None, "tp"))
    return jax.shard_map(body, mesh=mesh, in_specs=in_specs, out_specs=out_specs, check_vma=False)
```

```python
import jax
import jax.numpy as jnp
from jax import lax
from jax.experimental import pallas as pl
from jax.experimental.pallas import tpu as pltpu
from jax.sharding import PartitionSpec as P

HD = 128


rope_base = 500000.0
norm_eps = 1e-06
masked_fill = -1e30


RELATIVE = ("own", "ax", "aup", "adn", "m1", "m2", "m3", "m4")


def tp_links(width):
    size = 8
    cross = [(i, i ^ 1) for i in range(size)]
    up = [(i, (i + 2) % size) for i in range(size)]
    down = [(i, (i - 2) % size) for i in range(size)]
    t = lax.axis_index("tp")
    y, x = t // 2, t % 2
    other = 1 - x

    def block(dy, side):
        return ((y + dy) % 4) * 2 + side

    order = {
        "own": block(0, x), "ax": block(0, other), "aup": block(-1, x), "adn": block(1, x),
        "m1": block(1, other), "m2": block(-1, other), "m3": block(2, x), "m4": block(2, other),
    }
    return cross, up, down, order


def tp_gather(piece):
    width = piece.shape[1]
    half, quarter = width // 2, width // 4
    cross, up, down, order = tp_links(width)
    send = lambda value, perm: lax.ppermute(value, "tp", perm)
    ax = send(piece, cross)
    aup = send(piece, up)
    adn = send(piece, down)
    bx = send(jnp.concatenate([adn[:, :half], aup[:, :half]], 1), cross)
    bdn = send(jnp.concatenate([ax[:, half:], adn[:, :half]], 1), down)
    bup = send(jnp.concatenate([ax[:, half:], aup[:, half:]], 1), up)
    m1 = jnp.concatenate([bx[:, :half], bdn[:, :half]], 1)
    m2 = jnp.concatenate([bx[:, half:], bup[:, :half]], 1)
    m3 = jnp.concatenate([bdn[:, half:], bup[:, half:]], 1)
    cx = send(m3[:, :half], cross)
    cdn = send(m1[:, half:half + quarter], down)
    cup = send(m2[:, half + quarter:], up)
    m4 = jnp.concatenate([cx, cdn, cup], 1)
    return [[piece, ax, aup, adn], [m1, m2, m3], [m4]], order


def tp_reduce_scatter(b, width):
    half, quarter = width // 2, width // 4
    cross, up, down, order = tp_links(width)
    send = lambda value, perm: lax.ppermute(value.astype(jnp.bfloat16), "tp", perm).astype(jnp.float32)
    rx = send(b["m4"][:, :half], cross)
    rup = send(b["m4"][:, half:half + quarter], up)
    rdn = send(b["m4"][:, half + quarter:], down)
    m1, m2, m3 = b["m1"], b["m2"], b["m3"]
    m3 = jnp.concatenate([m3[:, :half] + rx, m3[:, half:]], 1)
    m1 = jnp.concatenate([m1[:, :half], m1[:, half:half + quarter] + rup, m1[:, half + quarter:]], 1)
    m2 = jnp.concatenate([m2[:, :half + quarter], m2[:, half + quarter:] + rdn], 1)
    rx = send(jnp.concatenate([m1[:, :half], m2[:, :half]], 1), cross)
    rup = send(jnp.concatenate([m1[:, half:], m3[:, :half]], 1), up)
    rdn = send(jnp.concatenate([m2[:, half:], m3[:, half:]], 1), down)
    ax = jnp.concatenate([b["ax"][:, :half], b["ax"][:, half:] + rup[:, :half] + rdn[:, :half]], 1)
    adn = jnp.concatenate([b["adn"][:, :half] + rx[:, :half] + rup[:, half:], b["adn"][:, half:]], 1)
    aup = jnp.concatenate([b["aup"][:, :half] + rx[:, half:], b["aup"][:, half:] + rdn[:, half:]], 1)
    return b["own"] + send(ax, cross) + send(adn, up) + send(aup, down)


def tp_sum(values):
    for bit in (1, 2, 4):
        values = jax.tree.map(
            lambda v, bit=bit: v + lax.ppermute(v, "tp", [(i, i ^ bit) for i in range(8)]), values
        )
    return values


def rope_pack(proj, square, gains, cosine, sine, seqs, pos_dev, full_width):
    _, rows, width = proj.shape
    heads = width // HD

    def kernel(proj_ref, square_ref, gain_ref, cos_ref, sin_ref, pack_ref, fresh_ref):
        cos_v = cos_ref[...]
        sin_v = sin_ref[...]
        for c in range(3):
            x = proj_ref[c]
            if c < 2:
                x = x * lax.rsqrt(square_ref[c] / full_width + norm_eps) * gain_ref[c]
            for h in range(heads):
                xh = x[:, h * HD:(h + 1) * HD]
                if c < 2:
                    xh = xh * cos_v + pltpu.roll(xh, HD // 2, 1) * sin_v
                xh = xh.astype(jnp.bfloat16)
                if c < 2:
                    for b in range(seqs):
                        pack_ref[b * heads + h, c] = xh[b * pos_dev:(b + 1) * pos_dev]
                fresh_ref[c, :, h * HD:(h + 1) * HD] = xh[seqs * pos_dev:].astype(jnp.float32)

    return pl.pallas_call(
        kernel,
        out_shape=(
            jax.ShapeDtypeStruct((seqs * heads, 2, pos_dev, HD), jnp.bfloat16),
            jax.ShapeDtypeStruct((3, rows - seqs * pos_dev, width), jnp.float32),
        ),
    )(proj, square, gains, cosine, sine)


def attend_pair(q_all, k_all, v_all, q_new, k_new, v_new, length):
    count = q_all.shape[0]
    scale = HD ** (-0.5)
    bounds = (0, count // 4, count // 2, count * 3 // 4, count)
    outs = []
    for begin, stop in zip(bounds[:-1], bounds[1:]):
        scores = (
            jnp.dot(q_all[begin:stop], k_all[:stop].T, preferred_element_type=jnp.float32)
            * scale
        )
        query_pos = begin + jnp.arange(stop - begin, dtype=jnp.int32)[:, None]
        key_pos = jnp.arange(stop, dtype=jnp.int32)[None, :]
        valid = (key_pos <= query_pos) & (key_pos < length)
        scores = jnp.where(valid, scores, masked_fill)
        top = jnp.max(scores, -1, keepdims=True)
        weights = jnp.where(valid, jnp.exp(scores - top), 0.0)
        total = jnp.sum(weights, -1, keepdims=True)
        outs.append(
            jnp.dot(weights.astype(jnp.bfloat16), v_all[:stop], preferred_element_type=jnp.float32)
            / total
        )
    prompt_out = jnp.concatenate(outs, 0).astype(jnp.bfloat16)
    new_scores = jnp.dot(k_all, q_new, preferred_element_type=jnp.float32) * scale
    live = jnp.arange(count, dtype=jnp.int32) < length
    new_scores = jnp.where(live, new_scores, masked_fill)
    self_score = jnp.dot(q_new, k_new, preferred_element_type=jnp.float32) * scale
    new_top = jnp.maximum(jnp.max(new_scores), self_score)
    new_weights = jnp.where(live, jnp.exp(new_scores - new_top), 0.0)
    own_weight = jnp.exp(self_score - new_top)
    new_total = jnp.sum(new_weights) + own_weight
    own_rounded = lax.optimization_barrier(own_weight.astype(jnp.bfloat16)).astype(jnp.float32)
    numer = jnp.dot(new_weights.astype(jnp.bfloat16), v_all, preferred_element_type=jnp.float32)
    numer = numer + own_rounded * v_new.astype(jnp.float32)
    return prompt_out, (numer / new_total).astype(jnp.bfloat16)


def body(tokens, new_tokens, w_qkv, w_out, q_gain, k_gain, post_gain, lengths):
    seqs, pos_dev, width_local = tokens.shape
    heads_local = width_local // HD
    full_width = w_qkv.shape[1]
    n_seq = lax.axis_size("seq")
    pairs = seqs * heads_local
    assert pairs == n_seq
    prompt_rows = seqs * pos_dev
    full_len = pos_dev * n_seq
    flat_rows = tokens.reshape(prompt_rows, width_local)
    local_rows = jnp.concatenate([flat_rows, new_tokens], 0)
    rounds, order = tp_gather(local_rows)

    def in_relative_order(weight, axis):
        return [
            lax.dynamic_slice_in_dim(weight, order[name] * width_local, width_local, axis)
            for name in RELATIVE
        ]

    w_blocks = in_relative_order(w_qkv, 1)
    proj, start = None, 0
    for blocks in rounds:
        stop = start + len(blocks)
        term = jnp.einsum(
            "tn,cnf->ctf",
            jnp.concatenate(blocks, 1),
            jnp.concatenate(w_blocks[start:stop], 1),
            preferred_element_type=jnp.float32,
        )
        proj = term if proj is None else proj + term
        start = stop
    query_raw, key_raw = proj[0], proj[1]
    value_pack = proj[2, :prompt_rows].astype(jnp.bfloat16).reshape(seqs, pos_dev, heads_local, HD)
    value_pack = value_pack.transpose(0, 2, 1, 3).reshape(pairs, pos_dev, HD)
    value_all = lax.all_to_all(value_pack, "seq", 0, 0, tiled=True).reshape(full_len, HD)
    squares = tp_sum(jnp.stack([jnp.sum(query_raw * query_raw, -1), jnp.sum(key_raw * key_raw, -1)]))

    seq_index = lax.axis_index("seq")
    query_pos = seq_index * pos_dev + jnp.arange(pos_dev, dtype=jnp.int32)
    row_pos = jnp.concatenate([jnp.tile(query_pos, seqs), lengths.astype(jnp.int32)], 0)
    half = HD // 2
    freq = rope_base ** (-(jnp.arange(half, dtype=jnp.float32) * 2.0) / HD)
    angle = row_pos.astype(jnp.float32)[:, None] * freq
    cosine, sine = jnp.cos(angle), jnp.sin(angle)
    qkv, fresh = rope_pack(
        proj,
        squares[:, :, None],
        jnp.stack([q_gain, k_gain])[:, None, :],
        jnp.concatenate([cosine, cosine], 1),
        jnp.concatenate([-sine, sine], 1),
        seqs,
        pos_dev,
        full_width,
    )

    got = lax.all_to_all(qkv, "seq", 0, 0, tiled=True)
    full = got.transpose(1, 0, 2, 3).reshape(2, full_len, HD)

    owner = seq_index
    own_prompt = owner // heads_local
    fresh = fresh.astype(jnp.bfloat16).reshape(3, pairs, HD)
    new_q, new_k, new_v = fresh[0, owner], fresh[1, owner], fresh[2, owner]
    prompt_out, new_out = attend_pair(
        full[0], full[1], value_all, new_q, new_k, new_v, lengths[own_prompt]
    )

    pad = 8
    back = jnp.concatenate(
        [prompt_out.reshape(n_seq, pos_dev, HD), jnp.broadcast_to(new_out, (n_seq, pad, HD))], 1
    )
    ret = lax.all_to_all(back, "seq", 0, 0, tiled=True)
    ret = ret.reshape(seqs, heads_local, pos_dev + pad, HD)
    attn_rows = ret[:, :, :pos_dev].transpose(0, 2, 1, 3).reshape(prompt_rows, width_local)
    attn_new = ret[:, :, pos_dev].reshape(seqs, width_local)
    attention = jnp.concatenate([attn_rows, attn_new], 0)

    wo_blocks = in_relative_order(w_out, 1)
    part = {}
    for names in (RELATIVE[7:], RELATIVE[4:7], RELATIVE[:4]):
        columns = [wo_blocks[RELATIVE.index(name)] for name in names]
        value = jnp.dot(attention, jnp.concatenate(columns, 1), preferred_element_type=jnp.float32)
        for i, name in enumerate(names):
            part[name] = value[:, i * width_local:(i + 1) * width_local]
    summed = tp_reduce_scatter(part, width_local)
    square = tp_sum(jnp.sum(summed * summed, -1))
    out = (
        local_rows.astype(jnp.float32)
        + summed * lax.rsqrt(square[:, None] / full_width + norm_eps) * post_gain
    ).astype(jnp.bfloat16)
    return (
        out[:prompt_rows].reshape(seqs, pos_dev, width_local),
        out[prompt_rows:],
    )


def solution(mesh):
    in_specs = (
        P(None, "seq", "tp"),
        P(None, "tp"),
        P(None, None, "tp"),
        P("tp", None),
        P("tp"),
        P("tp"),
        P("tp"),
        P(),
    )
    out_specs = (P(None, "seq", "tp"), P(None, "tp"))
    return jax.shard_map(body, mesh=mesh, in_specs=in_specs, out_specs=out_specs, check_vma=False)
```

```python
import jax
import jax.numpy as jnp
from jax import lax
from jax.experimental import pallas as pl
from jax.experimental.pallas import tpu as pltpu
from jax.sharding import PartitionSpec as P

HD = 128


rope_base = 500000.0
norm_eps = 1e-06
masked_fill = -1e30


RELATIVE = ("own", "ax", "aup", "adn", "m1", "m2", "m3", "m4")


def tp_links(width):
    size = 8
    cross = [(i, i ^ 1) for i in range(size)]
    up = [(i, (i + 2) % size) for i in range(size)]
    down = [(i, (i - 2) % size) for i in range(size)]
    t = lax.axis_index("tp")
    y, x = t // 2, t % 2
    other = 1 - x

    def block(dy, side):
        return ((y + dy) % 4) * 2 + side

    order = {
        "own": block(0, x), "ax": block(0, other), "aup": block(-1, x), "adn": block(1, x),
        "m1": block(1, other), "m2": block(-1, other), "m3": block(2, x), "m4": block(2, other),
    }
    return cross, up, down, order


def tp_gather(piece):
    width = piece.shape[1]
    half, quarter = width // 2, width // 4
    cross, up, down, order = tp_links(width)
    send = lambda value, perm: lax.ppermute(value, "tp", perm)
    ax = send(piece, cross)
    aup = send(piece, up)
    adn = send(piece, down)
    bx = send(jnp.concatenate([adn[:, :half], aup[:, :half]], 1), cross)
    bdn = send(jnp.concatenate([ax[:, half:], adn[:, :half]], 1), down)
    bup = send(jnp.concatenate([ax[:, half:], aup[:, half:]], 1), up)
    m1 = jnp.concatenate([bx[:, :half], bdn[:, :half]], 1)
    m2 = jnp.concatenate([bx[:, half:], bup[:, :half]], 1)
    m3 = jnp.concatenate([bdn[:, half:], bup[:, half:]], 1)
    cx = send(m3[:, :half], cross)
    cdn = send(m1[:, half:half + quarter], down)
    cup = send(m2[:, half + quarter:], up)
    m4 = jnp.concatenate([cx, cdn, cup], 1)
    return [[piece, ax, aup, adn], [m1, m2, m3], [m4]], order


def tp_reduce_scatter(b, width):
    half, quarter = width // 2, width // 4
    cross, up, down, order = tp_links(width)
    send = lambda value, perm: lax.ppermute(value.astype(jnp.bfloat16), "tp", perm).astype(jnp.float32)
    rx = send(b["m4"][:, :half], cross)
    rup = send(b["m4"][:, half:half + quarter], up)
    rdn = send(b["m4"][:, half + quarter:], down)
    m1, m2, m3 = b["m1"], b["m2"], b["m3"]
    m3 = jnp.concatenate([m3[:, :half] + rx, m3[:, half:]], 1)
    m1 = jnp.concatenate([m1[:, :half], m1[:, half:half + quarter] + rup, m1[:, half + quarter:]], 1)
    m2 = jnp.concatenate([m2[:, :half + quarter], m2[:, half + quarter:] + rdn], 1)
    rx = send(jnp.concatenate([m1[:, :half], m2[:, :half]], 1), cross)
    rup = send(jnp.concatenate([m1[:, half:], m3[:, :half]], 1), up)
    rdn = send(jnp.concatenate([m2[:, half:], m3[:, half:]], 1), down)
    ax = jnp.concatenate([b["ax"][:, :half], b["ax"][:, half:] + rup[:, :half] + rdn[:, :half]], 1)
    adn = jnp.concatenate([b["adn"][:, :half] + rx[:, :half] + rup[:, half:], b["adn"][:, half:]], 1)
    aup = jnp.concatenate([b["aup"][:, :half] + rx[:, half:], b["aup"][:, half:] + rdn[:, half:]], 1)
    return b["own"] + send(ax, cross) + send(adn, up) + send(aup, down)


def tp_sum(values):
    size = 8
    column = values
    for shift in (2, -2, 4):
        column = column + lax.ppermute(values, "tp", [(i, (i + shift) % size) for i in range(size)])
    return column + lax.ppermute(column, "tp", [(i, i ^ 1) for i in range(size)])


def rope_pack(proj, square, gains, cosine, sine, seqs, pos_dev, full_width):
    _, rows, width = proj.shape
    heads = width // HD

    def kernel(proj_ref, square_ref, gain_ref, cos_ref, sin_ref, pack_ref, fresh_ref):
        cos_v = cos_ref[...]
        sin_v = sin_ref[...]
        for c in range(3):
            x = proj_ref[c]
            if c < 2:
                x = x * lax.rsqrt(square_ref[c] / full_width + norm_eps) * gain_ref[c]
            for h in range(heads):
                xh = x[:, h * HD:(h + 1) * HD]
                if c < 2:
                    xh = xh * cos_v + pltpu.roll(xh, HD // 2, 1) * sin_v
                xh = xh.astype(jnp.bfloat16)
                for b in range(seqs):
                    pack_ref[b * heads + h, c] = xh[b * pos_dev:(b + 1) * pos_dev]
                fresh_ref[c, :, h * HD:(h + 1) * HD] = xh[seqs * pos_dev:].astype(jnp.float32)

    return pl.pallas_call(
        kernel,
        out_shape=(
            jax.ShapeDtypeStruct((seqs * heads, 3, pos_dev, HD), jnp.bfloat16),
            jax.ShapeDtypeStruct((3, rows - seqs * pos_dev, width), jnp.float32),
        ),
    )(proj, square, gains, cosine, sine)


def attend_pair(q_all, k_all, v_all, q_new, k_new, v_new, length):
    count = q_all.shape[0]
    scale = HD ** (-0.5)
    bounds = (0, count // 4, count // 2, count * 3 // 4, count)
    outs = []
    for begin, stop in zip(bounds[:-1], bounds[1:]):
        scores = (
            jnp.dot(q_all[begin:stop], k_all[:stop].T, preferred_element_type=jnp.float32)
            * scale
        )
        query_pos = begin + jnp.arange(stop - begin, dtype=jnp.int32)[:, None]
        key_pos = jnp.arange(stop, dtype=jnp.int32)[None, :]
        valid = (key_pos <= query_pos) & (key_pos < length)
        scores = jnp.where(valid, scores, masked_fill)
        top = jnp.max(scores, -1, keepdims=True)
        weights = jnp.where(valid, jnp.exp(scores - top), 0.0)
        total = jnp.sum(weights, -1, keepdims=True)
        outs.append(
            jnp.dot(weights.astype(jnp.bfloat16), v_all[:stop], preferred_element_type=jnp.float32)
            / total
        )
    prompt_out = jnp.concatenate(outs, 0).astype(jnp.bfloat16)
    new_scores = jnp.dot(k_all, q_new, preferred_element_type=jnp.float32) * scale
    live = jnp.arange(count, dtype=jnp.int32) < length
    new_scores = jnp.where(live, new_scores, masked_fill)
    self_score = jnp.dot(q_new, k_new, preferred_element_type=jnp.float32) * scale
    new_top = jnp.maximum(jnp.max(new_scores), self_score)
    new_weights = jnp.where(live, jnp.exp(new_scores - new_top), 0.0)
    own_weight = jnp.exp(self_score - new_top)
    new_total = jnp.sum(new_weights) + own_weight
    own_rounded = lax.optimization_barrier(own_weight.astype(jnp.bfloat16)).astype(jnp.float32)
    numer = jnp.dot(new_weights.astype(jnp.bfloat16), v_all, preferred_element_type=jnp.float32)
    numer = numer + own_rounded * v_new.astype(jnp.float32)
    return prompt_out, (numer / new_total).astype(jnp.bfloat16)


def body(tokens, new_tokens, w_qkv, w_out, q_gain, k_gain, post_gain, lengths):
    seqs, pos_dev, width_local = tokens.shape
    heads_local = width_local // HD
    full_width = w_qkv.shape[1]
    n_seq = lax.axis_size("seq")
    pairs = seqs * heads_local
    assert pairs == n_seq
    prompt_rows = seqs * pos_dev
    full_len = pos_dev * n_seq
    flat_rows = tokens.reshape(prompt_rows, width_local)
    local_rows = jnp.concatenate([flat_rows, new_tokens], 0)
    rounds, order = tp_gather(local_rows)

    def in_relative_order(weight, axis):
        return [
            lax.dynamic_slice_in_dim(weight, order[name] * width_local, width_local, axis)
            for name in RELATIVE
        ]

    w_blocks = in_relative_order(w_qkv, 1)
    proj, start = None, 0
    for blocks in rounds:
        stop = start + len(blocks)
        term = jnp.einsum(
            "tn,cnf->ctf",
            jnp.concatenate(blocks, 1),
            jnp.concatenate(w_blocks[start:stop], 1),
            preferred_element_type=jnp.float32,
        )
        proj = term if proj is None else proj + term
        start = stop
    query_raw, key_raw = proj[0], proj[1]
    squares = tp_sum(jnp.stack([jnp.sum(query_raw * query_raw, -1), jnp.sum(key_raw * key_raw, -1)]))

    seq_index = lax.axis_index("seq")
    query_pos = seq_index * pos_dev + jnp.arange(pos_dev, dtype=jnp.int32)
    row_pos = jnp.concatenate([jnp.tile(query_pos, seqs), lengths.astype(jnp.int32)], 0)
    half = HD // 2
    freq = rope_base ** (-(jnp.arange(half, dtype=jnp.float32) * 2.0) / HD)
    angle = row_pos.astype(jnp.float32)[:, None] * freq
    cosine, sine = jnp.cos(angle), jnp.sin(angle)
    qkv, fresh = rope_pack(
        proj,
        squares[:, :, None],
        jnp.stack([q_gain, k_gain])[:, None, :],
        jnp.concatenate([cosine, cosine], 1),
        jnp.concatenate([-sine, sine], 1),
        seqs,
        pos_dev,
        full_width,
    )

    got = lax.all_to_all(qkv, "seq", 0, 0, tiled=True)
    full = got.transpose(1, 0, 2, 3).reshape(3, full_len, HD)

    owner = seq_index
    own_prompt = owner // heads_local
    fresh = fresh.astype(jnp.bfloat16).reshape(3, pairs, HD)
    new_q, new_k, new_v = fresh[0, owner], fresh[1, owner], fresh[2, owner]
    prompt_out, new_out = attend_pair(
        full[0], full[1], full[2], new_q, new_k, new_v, lengths[own_prompt]
    )

    pad = 8
    back = jnp.concatenate(
        [prompt_out.reshape(n_seq, pos_dev, HD), jnp.broadcast_to(new_out, (n_seq, pad, HD))], 1
    )
    ret = lax.all_to_all(back, "seq", 0, 0, tiled=True)
    ret = ret.reshape(seqs, heads_local, pos_dev + pad, HD)
    attn_rows = ret[:, :, :pos_dev].transpose(0, 2, 1, 3).reshape(prompt_rows, width_local)
    attn_new = ret[:, :, pos_dev].reshape(seqs, width_local)
    attention = jnp.concatenate([attn_rows, attn_new], 0)

    wo_blocks = in_relative_order(w_out, 1)
    part = {}
    for names in (RELATIVE[7:], RELATIVE[4:7], RELATIVE[:4]):
        columns = [wo_blocks[RELATIVE.index(name)] for name in names]
        value = jnp.dot(attention, jnp.concatenate(columns, 1), preferred_element_type=jnp.float32)
        for i, name in enumerate(names):
            part[name] = value[:, i * width_local:(i + 1) * width_local]
    summed = tp_reduce_scatter(part, width_local)
    square = tp_sum(jnp.sum(summed * summed, -1))
    out = (
        local_rows.astype(jnp.float32)
        + summed * lax.rsqrt(square[:, None] / full_width + norm_eps) * post_gain
    ).astype(jnp.bfloat16)
    return (
        out[:prompt_rows].reshape(seqs, pos_dev, width_local),
        out[prompt_rows:],
    )


def solution(mesh):
    in_specs = (
        P(None, "seq", "tp"),
        P(None, "tp"),
        P(None, None, "tp"),
        P("tp", None),
        P("tp"),
        P("tp"),
        P("tp"),
        P(),
    )
    out_specs = (P(None, "seq", "tp"), P(None, "tp"))
    return jax.shard_map(body, mesh=mesh, in_specs=in_specs, out_specs=out_specs, check_vma=False)
```

```python
import jax
import jax.numpy as jnp
from jax import lax
from jax.experimental import pallas as pl
from jax.experimental.pallas import tpu as pltpu
from jax.sharding import PartitionSpec as P

HD = 128


rope_base = 500000.0
norm_eps = 1e-06
masked_fill = -1e30


RELATIVE = ("own", "ax", "aup", "adn", "m1", "m2", "m3", "m4")


def tp_links(width):
    size = 8
    cross = [(i, i ^ 1) for i in range(size)]
    up = [(i, (i + 2) % size) for i in range(size)]
    down = [(i, (i - 2) % size) for i in range(size)]
    t = lax.axis_index("tp")
    y, x = t // 2, t % 2
    other = 1 - x

    def block(dy, side):
        return ((y + dy) % 4) * 2 + side

    order = {
        "own": block(0, x), "ax": block(0, other), "aup": block(-1, x), "adn": block(1, x),
        "m1": block(1, other), "m2": block(-1, other), "m3": block(2, x), "m4": block(2, other),
    }
    return cross, up, down, order


def tp_gather(piece):
    width = piece.shape[1]
    half, quarter = width // 2, width // 4
    cross, up, down, order = tp_links(width)
    send = lambda value, perm: lax.ppermute(value, "tp", perm)
    ax = send(piece, cross)
    aup = send(piece, up)
    adn = send(piece, down)
    bx = send(jnp.concatenate([adn[:, :half], aup[:, :half]], 1), cross)
    bdn = send(jnp.concatenate([ax[:, half:], adn[:, :half]], 1), down)
    bup = send(jnp.concatenate([ax[:, half:], aup[:, half:]], 1), up)
    m1 = jnp.concatenate([bx[:, :half], bdn[:, :half]], 1)
    m2 = jnp.concatenate([bx[:, half:], bup[:, :half]], 1)
    m3 = jnp.concatenate([bdn[:, half:], bup[:, half:]], 1)
    cx = send(m3[:, :half], cross)
    cdn = send(m1[:, half:half + quarter], down)
    cup = send(m2[:, half + quarter:], up)
    m4 = jnp.concatenate([cx, cdn, cup], 1)
    return [[piece, ax, aup, adn], [m1, m2, m3], [m4]], order


def tp_reduce_scatter(b, width):
    half, quarter = width // 2, width // 4
    cross, up, down, order = tp_links(width)
    send = lambda value, perm: lax.ppermute(value.astype(jnp.bfloat16), "tp", perm).astype(jnp.float32)
    rx = send(b["m4"][:, :half], cross)
    rup = send(b["m4"][:, half:half + quarter], up)
    rdn = send(b["m4"][:, half + quarter:], down)
    m1, m2, m3 = b["m1"], b["m2"], b["m3"]
    m3 = jnp.concatenate([m3[:, :half] + rx, m3[:, half:]], 1)
    m1 = jnp.concatenate([m1[:, :half], m1[:, half:half + quarter] + rup, m1[:, half + quarter:]], 1)
    m2 = jnp.concatenate([m2[:, :half + quarter], m2[:, half + quarter:] + rdn], 1)
    rx = send(jnp.concatenate([m1[:, :half], m2[:, :half]], 1), cross)
    rup = send(jnp.concatenate([m1[:, half:], m3[:, :half]], 1), up)
    rdn = send(jnp.concatenate([m2[:, half:], m3[:, half:]], 1), down)
    ax = jnp.concatenate([b["ax"][:, :half], b["ax"][:, half:] + rup[:, :half] + rdn[:, :half]], 1)
    adn = jnp.concatenate([b["adn"][:, :half] + rx[:, :half] + rup[:, half:], b["adn"][:, half:]], 1)
    aup = jnp.concatenate([b["aup"][:, :half] + rx[:, half:], b["aup"][:, half:] + rdn[:, half:]], 1)
    return b["own"] + send(ax, cross) + send(adn, up) + send(aup, down)


def tp_sum(values):
    size = 8
    column = values
    for shift in (2, -2, 4):
        column = column + lax.ppermute(values, "tp", [(i, (i + shift) % size) for i in range(size)])
    return column + lax.ppermute(column, "tp", [(i, i ^ 1) for i in range(size)])


def rope_pack(proj, square, gains, cosine, sine, seqs, pos_dev, full_width):
    _, rows, width = proj.shape
    heads = width // HD

    def kernel(proj_ref, square_ref, gain_ref, cos_ref, sin_ref, pack_ref, fresh_ref):
        cos_v = cos_ref[...]
        sin_v = sin_ref[...]
        for c in range(3):
            x = proj_ref[c]
            if c < 2:
                x = x * lax.rsqrt(square_ref[c] / full_width + norm_eps) * gain_ref[c]
            for h in range(heads):
                xh = x[:, h * HD:(h + 1) * HD]
                if c < 2:
                    xh = xh * cos_v + pltpu.roll(xh, HD // 2, 1) * sin_v
                xh = xh.astype(jnp.bfloat16)
                for b in range(seqs):
                    pack_ref[b * heads + h, c] = xh[b * pos_dev:(b + 1) * pos_dev]
                fresh_ref[c, :, h * HD:(h + 1) * HD] = xh[seqs * pos_dev:].astype(jnp.float32)

    return pl.pallas_call(
        kernel,
        out_shape=(
            jax.ShapeDtypeStruct((seqs * heads, 3, pos_dev, HD), jnp.bfloat16),
            jax.ShapeDtypeStruct((3, rows - seqs * pos_dev, width), jnp.float32),
        ),
    )(proj, square, gains, cosine, sine)


def attend_pair(q_all, k_all, v_all, q_new, k_new, v_new, length):
    count = q_all.shape[0]
    scale = HD ** (-0.5)
    bounds = (0, count // 2, count)
    outs = []
    for begin, stop in zip(bounds[:-1], bounds[1:]):
        scores = (
            jnp.dot(q_all[begin:stop], k_all[:stop].T, preferred_element_type=jnp.float32)
            * scale
        )
        query_pos = begin + jnp.arange(stop - begin, dtype=jnp.int32)[:, None]
        key_pos = jnp.arange(stop, dtype=jnp.int32)[None, :]
        valid = (key_pos <= query_pos) & (key_pos < length)
        scores = jnp.where(valid, scores, masked_fill)
        top = jnp.max(scores, -1, keepdims=True)
        weights = jnp.where(valid, jnp.exp(scores - top), 0.0)
        total = jnp.sum(weights, -1, keepdims=True)
        outs.append(
            jnp.dot(weights.astype(jnp.bfloat16), v_all[:stop], preferred_element_type=jnp.float32)
            / total
        )
    prompt_out = jnp.concatenate(outs, 0).astype(jnp.bfloat16)
    new_scores = jnp.dot(k_all, q_new, preferred_element_type=jnp.float32) * scale
    live = jnp.arange(count, dtype=jnp.int32) < length
    new_scores = jnp.where(live, new_scores, masked_fill)
    self_score = jnp.dot(q_new, k_new, preferred_element_type=jnp.float32) * scale
    new_top = jnp.maximum(jnp.max(new_scores), self_score)
    new_weights = jnp.where(live, jnp.exp(new_scores - new_top), 0.0)
    own_weight = jnp.exp(self_score - new_top)
    new_total = jnp.sum(new_weights) + own_weight
    own_rounded = lax.optimization_barrier(own_weight.astype(jnp.bfloat16)).astype(jnp.float32)
    numer = jnp.dot(new_weights.astype(jnp.bfloat16), v_all, preferred_element_type=jnp.float32)
    numer = numer + own_rounded * v_new.astype(jnp.float32)
    return prompt_out, (numer / new_total).astype(jnp.bfloat16)


def body(tokens, new_tokens, w_qkv, w_out, q_gain, k_gain, post_gain, lengths):
    seqs, pos_dev, width_local = tokens.shape
    heads_local = width_local // HD
    full_width = w_qkv.shape[1]
    n_seq = lax.axis_size("seq")
    pairs = seqs * heads_local
    assert pairs == n_seq
    prompt_rows = seqs * pos_dev
    full_len = pos_dev * n_seq
    flat_rows = tokens.reshape(prompt_rows, width_local)
    local_rows = jnp.concatenate([flat_rows, new_tokens], 0)
    rounds, order = tp_gather(local_rows)

    def in_relative_order(weight, axis):
        return [
            lax.dynamic_slice_in_dim(weight, order[name] * width_local, width_local, axis)
            for name in RELATIVE
        ]

    w_blocks = in_relative_order(w_qkv, 1)
    proj, start = None, 0
    for blocks in rounds:
        stop = start + len(blocks)
        term = jnp.einsum(
            "tn,cnf->ctf",
            jnp.concatenate(blocks, 1),
            jnp.concatenate(w_blocks[start:stop], 1),
            preferred_element_type=jnp.float32,
        )
        proj = term if proj is None else proj + term
        start = stop
    query_raw, key_raw = proj[0], proj[1]
    squares = tp_sum(jnp.stack([jnp.sum(query_raw * query_raw, -1), jnp.sum(key_raw * key_raw, -1)]))

    seq_index = lax.axis_index("seq")
    query_pos = seq_index * pos_dev + jnp.arange(pos_dev, dtype=jnp.int32)
    row_pos = jnp.concatenate([jnp.tile(query_pos, seqs), lengths.astype(jnp.int32)], 0)
    half = HD // 2
    freq = rope_base ** (-(jnp.arange(half, dtype=jnp.float32) * 2.0) / HD)
    angle = row_pos.astype(jnp.float32)[:, None] * freq
    cosine, sine = jnp.cos(angle), jnp.sin(angle)
    qkv, fresh = rope_pack(
        proj,
        squares[:, :, None],
        jnp.stack([q_gain, k_gain])[:, None, :],
        jnp.concatenate([cosine, cosine], 1),
        jnp.concatenate([-sine, sine], 1),
        seqs,
        pos_dev,
        full_width,
    )

    got = lax.all_to_all(qkv, "seq", 0, 0, tiled=True)
    full = got.transpose(1, 0, 2, 3).reshape(3, full_len, HD)

    owner = seq_index
    own_prompt = owner // heads_local
    fresh = fresh.astype(jnp.bfloat16).reshape(3, pairs, HD)
    new_q, new_k, new_v = fresh[0, owner], fresh[1, owner], fresh[2, owner]
    prompt_out, new_out = attend_pair(
        full[0], full[1], full[2], new_q, new_k, new_v, lengths[own_prompt]
    )

    pad = 8
    back = jnp.concatenate(
        [prompt_out.reshape(n_seq, pos_dev, HD), jnp.broadcast_to(new_out, (n_seq, pad, HD))], 1
    )
    ret = lax.all_to_all(back, "seq", 0, 0, tiled=True)
    ret = ret.reshape(seqs, heads_local, pos_dev + pad, HD)
    attn_rows = ret[:, :, :pos_dev].transpose(0, 2, 1, 3).reshape(prompt_rows, width_local)
    attn_new = ret[:, :, pos_dev].reshape(seqs, width_local)
    attention = jnp.concatenate([attn_rows, attn_new], 0)

    wo_blocks = in_relative_order(w_out, 1)
    part = {}
    for names in (RELATIVE[7:], RELATIVE[4:7], RELATIVE[:4]):
        columns = [wo_blocks[RELATIVE.index(name)] for name in names]
        value = jnp.dot(attention, jnp.concatenate(columns, 1), preferred_element_type=jnp.float32)
        for i, name in enumerate(names):
            part[name] = value[:, i * width_local:(i + 1) * width_local]
    summed = tp_reduce_scatter(part, width_local)
    square = tp_sum(jnp.sum(summed * summed, -1))
    out = (
        local_rows.astype(jnp.float32)
        + summed * lax.rsqrt(square[:, None] / full_width + norm_eps) * post_gain
    ).astype(jnp.bfloat16)
    return (
        out[:prompt_rows].reshape(seqs, pos_dev, width_local),
        out[prompt_rows:],
    )


def solution(mesh):
    in_specs = (
        P(None, "seq", "tp"),
        P(None, "tp"),
        P(None, None, "tp"),
        P("tp", None),
        P("tp"),
        P("tp"),
        P("tp"),
        P(),
    )
    out_specs = (P(None, "seq", "tp"), P(None, "tp"))
    return jax.shard_map(body, mesh=mesh, in_specs=in_specs, out_specs=out_specs, check_vma=False)
```

```python
import jax
import jax.numpy as jnp
from jax import lax
from jax.experimental import pallas as pl
from jax.experimental.pallas import tpu as pltpu
from jax.sharding import PartitionSpec as P

HD = 128


rope_base = 500000.0
norm_eps = 1e-06
masked_fill = -1e30


RELATIVE = ("own", "ax", "aup", "adn", "m1", "m2", "m3", "m4")


def tp_links(width):
    size = 8
    cross = [(i, i ^ 1) for i in range(size)]
    up = [(i, (i + 2) % size) for i in range(size)]
    down = [(i, (i - 2) % size) for i in range(size)]
    t = lax.axis_index("tp")
    y, x = t // 2, t % 2
    other = 1 - x

    def block(dy, side):
        return ((y + dy) % 4) * 2 + side

    order = {
        "own": block(0, x), "ax": block(0, other), "aup": block(-1, x), "adn": block(1, x),
        "m1": block(1, other), "m2": block(-1, other), "m3": block(2, x), "m4": block(2, other),
    }
    return cross, up, down, order


def tp_gather(piece):
    width = piece.shape[1]
    half, quarter = width // 2, width // 4
    cross, up, down, order = tp_links(width)
    send = lambda value, perm: lax.ppermute(value, "tp", perm)
    ax = send(piece, cross)
    aup = send(piece, up)
    adn = send(piece, down)
    bx = send(jnp.concatenate([adn[:, :half], aup[:, :half]], 1), cross)
    bdn = send(jnp.concatenate([ax[:, half:], adn[:, :half]], 1), down)
    bup = send(jnp.concatenate([ax[:, half:], aup[:, half:]], 1), up)
    m1 = jnp.concatenate([bx[:, :half], bdn[:, :half]], 1)
    m2 = jnp.concatenate([bx[:, half:], bup[:, :half]], 1)
    m3 = jnp.concatenate([bdn[:, half:], bup[:, half:]], 1)
    cx = send(m3[:, :half], cross)
    cdn = send(m1[:, half:half + quarter], down)
    cup = send(m2[:, half + quarter:], up)
    m4 = jnp.concatenate([cx, cdn, cup], 1)
    return [[piece, ax, aup, adn], [m1, m2, m3], [m4]], order


def tp_reduce_scatter(b, width):
    half, quarter = width // 2, width // 4
    cross, up, down, order = tp_links(width)
    send = lambda value, perm: lax.ppermute(value.astype(jnp.bfloat16), "tp", perm).astype(jnp.float32)
    rx = send(b["m4"][:, :half], cross)
    rup = send(b["m4"][:, half:half + quarter], up)
    rdn = send(b["m4"][:, half + quarter:], down)
    m1, m2, m3 = b["m1"], b["m2"], b["m3"]
    m3 = jnp.concatenate([m3[:, :half] + rx, m3[:, half:]], 1)
    m1 = jnp.concatenate([m1[:, :half], m1[:, half:half + quarter] + rup, m1[:, half + quarter:]], 1)
    m2 = jnp.concatenate([m2[:, :half + quarter], m2[:, half + quarter:] + rdn], 1)
    rx = send(jnp.concatenate([m1[:, :half], m2[:, :half]], 1), cross)
    rup = send(jnp.concatenate([m1[:, half:], m3[:, :half]], 1), up)
    rdn = send(jnp.concatenate([m2[:, half:], m3[:, half:]], 1), down)
    ax = jnp.concatenate([b["ax"][:, :half], b["ax"][:, half:] + rup[:, :half] + rdn[:, :half]], 1)
    adn = jnp.concatenate([b["adn"][:, :half] + rx[:, :half] + rup[:, half:], b["adn"][:, half:]], 1)
    aup = jnp.concatenate([b["aup"][:, :half] + rx[:, half:], b["aup"][:, half:] + rdn[:, half:]], 1)
    return b["own"] + send(ax, cross) + send(adn, up) + send(aup, down)


def tp_sum(values):
    size = 8
    column = values
    for shift in (2, -2, 4):
        column = column + lax.ppermute(values, "tp", [(i, (i + shift) % size) for i in range(size)])
    return column + lax.ppermute(column, "tp", [(i, i ^ 1) for i in range(size)])


def tp_sum_doubling(values):
    for bit in (1, 2, 4):
        values = values + lax.ppermute(values, "tp", [(i, i ^ bit) for i in range(8)])
    return values


def rope_pack(proj, square, gains, cosine, sine, seqs, pos_dev, full_width):
    _, rows, width = proj.shape
    heads = width // HD

    def kernel(proj_ref, square_ref, gain_ref, cos_ref, sin_ref, pack_ref, fresh_ref):
        cos_v = cos_ref[...]
        sin_v = sin_ref[...]
        for c in range(3):
            x = proj_ref[c]
            if c < 2:
                x = x * lax.rsqrt(square_ref[c] / full_width + norm_eps) * gain_ref[c]
            for h in range(heads):
                xh = x[:, h * HD:(h + 1) * HD]
                if c < 2:
                    xh = xh * cos_v + pltpu.roll(xh, HD // 2, 1) * sin_v
                xh = xh.astype(jnp.bfloat16)
                for b in range(seqs):
                    pack_ref[b * heads + h, c] = xh[b * pos_dev:(b + 1) * pos_dev]
                fresh_ref[c, :, h * HD:(h + 1) * HD] = xh[seqs * pos_dev:].astype(jnp.float32)

    return pl.pallas_call(
        kernel,
        out_shape=(
            jax.ShapeDtypeStruct((seqs * heads, 3, pos_dev, HD), jnp.bfloat16),
            jax.ShapeDtypeStruct((3, rows - seqs * pos_dev, width), jnp.float32),
        ),
    )(proj, square, gains, cosine, sine)


def attend_pair(q_all, k_all, v_all, q_new, k_new, v_new, length):
    count = q_all.shape[0]
    scale = HD ** (-0.5)
    bounds = (0, count // 4, count // 2, count * 3 // 4, count)
    outs = []
    for begin, stop in zip(bounds[:-1], bounds[1:]):
        scores = (
            jnp.dot(q_all[begin:stop], k_all[:stop].T, preferred_element_type=jnp.float32)
            * scale
        )
        query_pos = begin + jnp.arange(stop - begin, dtype=jnp.int32)[:, None]
        key_pos = jnp.arange(stop, dtype=jnp.int32)[None, :]
        valid = (key_pos <= query_pos) & (key_pos < length)
        scores = jnp.where(valid, scores, masked_fill)
        top = jnp.max(scores, -1, keepdims=True)
        weights = jnp.where(valid, jnp.exp(scores - top), 0.0)
        total = jnp.sum(weights, -1, keepdims=True)
        outs.append(
            jnp.dot(weights.astype(jnp.bfloat16), v_all[:stop], preferred_element_type=jnp.float32)
            / total
        )
    prompt_out = jnp.concatenate(outs, 0).astype(jnp.bfloat16)
    new_scores = jnp.dot(k_all, q_new, preferred_element_type=jnp.float32) * scale
    live = jnp.arange(count, dtype=jnp.int32) < length
    new_scores = jnp.where(live, new_scores, masked_fill)
    self_score = jnp.dot(q_new, k_new, preferred_element_type=jnp.float32) * scale
    new_top = jnp.maximum(jnp.max(new_scores), self_score)
    new_weights = jnp.where(live, jnp.exp(new_scores - new_top), 0.0)
    own_weight = jnp.exp(self_score - new_top)
    new_total = jnp.sum(new_weights) + own_weight
    own_rounded = lax.optimization_barrier(own_weight.astype(jnp.bfloat16)).astype(jnp.float32)
    numer = jnp.dot(new_weights.astype(jnp.bfloat16), v_all, preferred_element_type=jnp.float32)
    numer = numer + own_rounded * v_new.astype(jnp.float32)
    return prompt_out, (numer / new_total).astype(jnp.bfloat16)


def body(tokens, new_tokens, w_qkv, w_out, q_gain, k_gain, post_gain, lengths):
    seqs, pos_dev, width_local = tokens.shape
    heads_local = width_local // HD
    full_width = w_qkv.shape[1]
    n_seq = lax.axis_size("seq")
    pairs = seqs * heads_local
    assert pairs == n_seq
    prompt_rows = seqs * pos_dev
    full_len = pos_dev * n_seq
    flat_rows = tokens.reshape(prompt_rows, width_local)
    local_rows = jnp.concatenate([flat_rows, new_tokens], 0)
    rounds, order = tp_gather(local_rows)

    def in_relative_order(weight, axis):
        return [
            lax.dynamic_slice_in_dim(weight, order[name] * width_local, width_local, axis)
            for name in RELATIVE
        ]

    w_blocks = in_relative_order(w_qkv, 1)
    proj, start = None, 0
    for blocks in rounds:
        stop = start + len(blocks)
        term = jnp.einsum(
            "tn,cnf->ctf",
            jnp.concatenate(blocks, 1),
            jnp.concatenate(w_blocks[start:stop], 1),
            preferred_element_type=jnp.float32,
        )
        proj = term if proj is None else proj + term
        start = stop
    query_raw, key_raw = proj[0], proj[1]
    squares = tp_sum(jnp.stack([jnp.sum(query_raw * query_raw, -1), jnp.sum(key_raw * key_raw, -1)]))

    seq_index = lax.axis_index("seq")
    query_pos = seq_index * pos_dev + jnp.arange(pos_dev, dtype=jnp.int32)
    row_pos = jnp.concatenate([jnp.tile(query_pos, seqs), lengths.astype(jnp.int32)], 0)
    half = HD // 2
    freq = rope_base ** (-(jnp.arange(half, dtype=jnp.float32) * 2.0) / HD)
    angle = row_pos.astype(jnp.float32)[:, None] * freq
    cosine, sine = jnp.cos(angle), jnp.sin(angle)
    qkv, fresh = rope_pack(
        proj,
        squares[:, :, None],
        jnp.stack([q_gain, k_gain])[:, None, :],
        jnp.concatenate([cosine, cosine], 1),
        jnp.concatenate([-sine, sine], 1),
        seqs,
        pos_dev,
        full_width,
    )

    got = lax.all_to_all(qkv, "seq", 0, 0, tiled=True)
    full = got.transpose(1, 0, 2, 3).reshape(3, full_len, HD)

    owner = seq_index
    own_prompt = owner // heads_local
    fresh = fresh.astype(jnp.bfloat16).reshape(3, pairs, HD)
    new_q, new_k, new_v = fresh[0, owner], fresh[1, owner], fresh[2, owner]
    prompt_out, new_out = attend_pair(
        full[0], full[1], full[2], new_q, new_k, new_v, lengths[own_prompt]
    )

    pad = 8
    back = jnp.concatenate(
        [prompt_out.reshape(n_seq, pos_dev, HD), jnp.broadcast_to(new_out, (n_seq, pad, HD))], 1
    )
    ret = lax.all_to_all(back, "seq", 0, 0, tiled=True)
    ret = ret.reshape(seqs, heads_local, pos_dev + pad, HD)
    attn_rows = ret[:, :, :pos_dev].transpose(0, 2, 1, 3).reshape(prompt_rows, width_local)
    attn_new = ret[:, :, pos_dev].reshape(seqs, width_local)
    attention = jnp.concatenate([attn_rows, attn_new], 0)

    wo_blocks = in_relative_order(w_out, 1)
    part = {}
    for names in (RELATIVE[7:], RELATIVE[4:7], RELATIVE[:4]):
        columns = [wo_blocks[RELATIVE.index(name)] for name in names]
        value = jnp.dot(attention, jnp.concatenate(columns, 1), preferred_element_type=jnp.float32)
        for i, name in enumerate(names):
            part[name] = value[:, i * width_local:(i + 1) * width_local]
    summed = tp_reduce_scatter(part, width_local)
    square = tp_sum_doubling(jnp.sum(summed * summed, -1))
    out = (
        local_rows.astype(jnp.float32)
        + summed * lax.rsqrt(square[:, None] / full_width + norm_eps) * post_gain
    ).astype(jnp.bfloat16)
    return (
        out[:prompt_rows].reshape(seqs, pos_dev, width_local),
        out[prompt_rows:],
    )


def solution(mesh):
    in_specs = (
        P(None, "seq", "tp"),
        P(None, "tp"),
        P(None, None, "tp"),
        P("tp", None),
        P("tp"),
        P("tp"),
        P("tp"),
        P(),
    )
    out_specs = (P(None, "seq", "tp"), P(None, "tp"))
    return jax.shard_map(body, mesh=mesh, in_specs=in_specs, out_specs=out_specs, check_vma=False)
```

```python
import jax
import jax.numpy as jnp
from jax import lax
from jax.experimental import pallas as pl
from jax.experimental.pallas import tpu as pltpu
from jax.sharding import PartitionSpec as P

HD = 128


rope_base = 500000.0
norm_eps = 1e-06
masked_fill = -1e30


RELATIVE = ("own", "ax", "aup", "adn", "m1", "m2", "m3", "m4")


def tp_links(width):
    size = 8
    cross = [(i, i ^ 1) for i in range(size)]
    up = [(i, (i + 2) % size) for i in range(size)]
    down = [(i, (i - 2) % size) for i in range(size)]
    t = lax.axis_index("tp")
    y, x = t // 2, t % 2
    other = 1 - x

    def block(dy, side):
        return ((y + dy) % 4) * 2 + side

    order = {
        "own": block(0, x), "ax": block(0, other), "aup": block(-1, x), "adn": block(1, x),
        "m1": block(1, other), "m2": block(-1, other), "m3": block(2, x), "m4": block(2, other),
    }
    return cross, up, down, order


def tp_gather(piece):
    width = piece.shape[1]
    half, quarter = width // 2, width // 4
    cross, up, down, order = tp_links(width)
    send = lambda value, perm: lax.ppermute(value, "tp", perm)
    ax = send(piece, cross)
    aup = send(piece, up)
    adn = send(piece, down)
    bx = send(jnp.concatenate([adn[:, :half], aup[:, :half]], 1), cross)
    bdn = send(jnp.concatenate([ax[:, half:], adn[:, :half]], 1), down)
    bup = send(jnp.concatenate([ax[:, half:], aup[:, half:]], 1), up)
    m1 = jnp.concatenate([bx[:, :half], bdn[:, :half]], 1)
    m2 = jnp.concatenate([bx[:, half:], bup[:, :half]], 1)
    m3 = jnp.concatenate([bdn[:, half:], bup[:, half:]], 1)
    cdn = send(m1[:, :half], down)
    cup = send(m2[:, half:], up)
    m4 = jnp.concatenate([cdn, cup], 1)
    return [[piece, ax, aup, adn], [m1, m2, m3], [m4]], order


def tp_reduce_scatter(b, width):
    half, quarter = width // 2, width // 4
    cross, up, down, order = tp_links(width)
    send = lambda value, perm: lax.ppermute(value.astype(jnp.bfloat16), "tp", perm).astype(jnp.float32)
    rup = send(b["m4"][:, :half], up)
    rdn = send(b["m4"][:, half:], down)
    m1, m2, m3 = b["m1"], b["m2"], b["m3"]
    m1 = jnp.concatenate([m1[:, :half] + rup, m1[:, half:]], 1)
    m2 = jnp.concatenate([m2[:, :half], m2[:, half:] + rdn], 1)
    rx = send(jnp.concatenate([m1[:, :half], m2[:, :half]], 1), cross)
    rup = send(jnp.concatenate([m1[:, half:], m3[:, :half]], 1), up)
    rdn = send(jnp.concatenate([m2[:, half:], m3[:, half:]], 1), down)
    ax = jnp.concatenate([b["ax"][:, :half], b["ax"][:, half:] + rup[:, :half] + rdn[:, :half]], 1)
    adn = jnp.concatenate([b["adn"][:, :half] + rx[:, :half] + rup[:, half:], b["adn"][:, half:]], 1)
    aup = jnp.concatenate([b["aup"][:, :half] + rx[:, half:], b["aup"][:, half:] + rdn[:, half:]], 1)
    return b["own"] + send(ax, cross) + send(adn, up) + send(aup, down)


def tp_sum(values):
    size = 8
    column = values
    for shift in (2, -2, 4):
        column = column + lax.ppermute(values, "tp", [(i, (i + shift) % size) for i in range(size)])
    return column + lax.ppermute(column, "tp", [(i, i ^ 1) for i in range(size)])


def rope_pack(proj, square, gains, cosine, sine, seqs, pos_dev, full_width):
    _, rows, width = proj.shape
    heads = width // HD

    def kernel(proj_ref, square_ref, gain_ref, cos_ref, sin_ref, pack_ref, fresh_ref):
        cos_v = cos_ref[...]
        sin_v = sin_ref[...]
        for c in range(3):
            x = proj_ref[c]
            if c < 2:
                x = x * lax.rsqrt(square_ref[c] / full_width + norm_eps) * gain_ref[c]
            for h in range(heads):
                xh = x[:, h * HD:(h + 1) * HD]
                if c < 2:
                    xh = xh * cos_v + pltpu.roll(xh, HD // 2, 1) * sin_v
                xh = xh.astype(jnp.bfloat16)
                for b in range(seqs):
                    pack_ref[b * heads + h, c] = xh[b * pos_dev:(b + 1) * pos_dev]
                fresh_ref[c, :, h * HD:(h + 1) * HD] = xh[seqs * pos_dev:].astype(jnp.float32)

    return pl.pallas_call(
        kernel,
        out_shape=(
            jax.ShapeDtypeStruct((seqs * heads, 3, pos_dev, HD), jnp.bfloat16),
            jax.ShapeDtypeStruct((3, rows - seqs * pos_dev, width), jnp.float32),
        ),
    )(proj, square, gains, cosine, sine)


def attend_pair(q_all, k_all, v_all, q_new, k_new, v_new, length):
    count = q_all.shape[0]
    scale = HD ** (-0.5)
    bounds = (0, count // 2, count)
    outs = []
    for begin, stop in zip(bounds[:-1], bounds[1:]):
        scores = (
            jnp.dot(q_all[begin:stop], k_all[:stop].T, preferred_element_type=jnp.float32)
            * scale
        )
        query_pos = begin + jnp.arange(stop - begin, dtype=jnp.int32)[:, None]
        key_pos = jnp.arange(stop, dtype=jnp.int32)[None, :]
        valid = (key_pos <= query_pos) & (key_pos < length)
        scores = jnp.where(valid, scores, masked_fill)
        top = jnp.max(scores, -1, keepdims=True)
        weights = jnp.where(valid, jnp.exp(scores - top), 0.0)
        total = jnp.sum(weights, -1, keepdims=True)
        outs.append(
            jnp.dot(weights.astype(jnp.bfloat16), v_all[:stop], preferred_element_type=jnp.float32)
            / total
        )
    prompt_out = jnp.concatenate(outs, 0).astype(jnp.bfloat16)
    new_scores = jnp.dot(k_all, q_new, preferred_element_type=jnp.float32) * scale
    live = jnp.arange(count, dtype=jnp.int32) < length
    new_scores = jnp.where(live, new_scores, masked_fill)
    self_score = jnp.dot(q_new, k_new, preferred_element_type=jnp.float32) * scale
    new_top = jnp.maximum(jnp.max(new_scores), self_score)
    new_weights = jnp.where(live, jnp.exp(new_scores - new_top), 0.0)
    own_weight = jnp.exp(self_score - new_top)
    new_total = jnp.sum(new_weights) + own_weight
    own_rounded = lax.optimization_barrier(own_weight.astype(jnp.bfloat16)).astype(jnp.float32)
    numer = jnp.dot(new_weights.astype(jnp.bfloat16), v_all, preferred_element_type=jnp.float32)
    numer = numer + own_rounded * v_new.astype(jnp.float32)
    return prompt_out, (numer / new_total).astype(jnp.bfloat16)


def body(tokens, new_tokens, w_qkv, w_out, q_gain, k_gain, post_gain, lengths):
    seqs, pos_dev, width_local = tokens.shape
    heads_local = width_local // HD
    full_width = w_qkv.shape[1]
    n_seq = lax.axis_size("seq")
    pairs = seqs * heads_local
    assert pairs == n_seq
    prompt_rows = seqs * pos_dev
    full_len = pos_dev * n_seq
    flat_rows = tokens.reshape(prompt_rows, width_local)
    local_rows = jnp.concatenate([flat_rows, new_tokens], 0)
    rounds, order = tp_gather(local_rows)

    def in_relative_order(weight, axis):
        return [
            lax.dynamic_slice_in_dim(weight, order[name] * width_local, width_local, axis)
            for name in RELATIVE
        ]

    w_blocks = in_relative_order(w_qkv, 1)
    proj, start = None, 0
    for blocks in rounds:
        stop = start + len(blocks)
        term = jnp.einsum(
            "tn,cnf->ctf",
            jnp.concatenate(blocks, 1),
            jnp.concatenate(w_blocks[start:stop], 1),
            preferred_element_type=jnp.float32,
        )
        proj = term if proj is None else proj + term
        start = stop
    query_raw, key_raw = proj[0], proj[1]
    squares = tp_sum(jnp.stack([jnp.sum(query_raw * query_raw, -1), jnp.sum(key_raw * key_raw, -1)]))

    seq_index = lax.axis_index("seq")
    query_pos = seq_index * pos_dev + jnp.arange(pos_dev, dtype=jnp.int32)
    row_pos = jnp.concatenate([jnp.tile(query_pos, seqs), lengths.astype(jnp.int32)], 0)
    half = HD // 2
    freq = rope_base ** (-(jnp.arange(half, dtype=jnp.float32) * 2.0) / HD)
    angle = row_pos.astype(jnp.float32)[:, None] * freq
    cosine, sine = jnp.cos(angle), jnp.sin(angle)
    qkv, fresh = rope_pack(
        proj,
        squares[:, :, None],
        jnp.stack([q_gain, k_gain])[:, None, :],
        jnp.concatenate([cosine, cosine], 1),
        jnp.concatenate([-sine, sine], 1),
        seqs,
        pos_dev,
        full_width,
    )

    got = lax.all_to_all(qkv, "seq", 0, 0, tiled=True)
    full = got.transpose(1, 0, 2, 3).reshape(3, full_len, HD)

    owner = seq_index
    own_prompt = owner // heads_local
    fresh = fresh.astype(jnp.bfloat16).reshape(3, pairs, HD)
    new_q, new_k, new_v = fresh[0, owner], fresh[1, owner], fresh[2, owner]
    prompt_out, new_out = attend_pair(
        full[0], full[1], full[2], new_q, new_k, new_v, lengths[own_prompt]
    )

    pad = 8
    back = jnp.concatenate(
        [prompt_out.reshape(n_seq, pos_dev, HD), jnp.broadcast_to(new_out, (n_seq, pad, HD))], 1
    )
    ret = lax.all_to_all(back, "seq", 0, 0, tiled=True)
    ret = ret.reshape(seqs, heads_local, pos_dev + pad, HD)
    attn_rows = ret[:, :, :pos_dev].transpose(0, 2, 1, 3).reshape(prompt_rows, width_local)
    attn_new = ret[:, :, pos_dev].reshape(seqs, width_local)
    attention = jnp.concatenate([attn_rows, attn_new], 0)

    wo_blocks = in_relative_order(w_out, 1)
    part = {}
    for names in (RELATIVE[7:], RELATIVE[4:7], RELATIVE[:4]):
        columns = [wo_blocks[RELATIVE.index(name)] for name in names]
        value = jnp.dot(attention, jnp.concatenate(columns, 1), preferred_element_type=jnp.float32)
        for i, name in enumerate(names):
            part[name] = value[:, i * width_local:(i + 1) * width_local]
    summed = tp_reduce_scatter(part, width_local)
    square = tp_sum(jnp.sum(summed * summed, -1))
    out = (
        local_rows.astype(jnp.float32)
        + summed * lax.rsqrt(square[:, None] / full_width + norm_eps) * post_gain
    ).astype(jnp.bfloat16)
    return (
        out[:prompt_rows].reshape(seqs, pos_dev, width_local),
        out[prompt_rows:],
    )


def solution(mesh):
    in_specs = (
        P(None, "seq", "tp"),
        P(None, "tp"),
        P(None, None, "tp"),
        P("tp", None),
        P("tp"),
        P("tp"),
        P("tp"),
        P(),
    )
    out_specs = (P(None, "seq", "tp"), P(None, "tp"))
    return jax.shard_map(body, mesh=mesh, in_specs=in_specs, out_specs=out_specs, check_vma=False)
```

```python
import jax
import jax.numpy as jnp
from jax import lax
from jax.experimental import pallas as pl
from jax.experimental.pallas import tpu as pltpu
from jax.sharding import PartitionSpec as P

HD = 128


rope_base = 500000.0
norm_eps = 1e-06
masked_fill = -1e30


RELATIVE = ("own", "ax", "aup", "adn", "m1", "m2", "m3", "m4")


def tp_links(width):
    size = 8
    cross = [(i, i ^ 1) for i in range(size)]
    up = [(i, (i + 2) % size) for i in range(size)]
    down = [(i, (i - 2) % size) for i in range(size)]
    t = lax.axis_index("tp")
    y, x = t // 2, t % 2
    other = 1 - x

    def block(dy, side):
        return ((y + dy) % 4) * 2 + side

    order = {
        "own": block(0, x), "ax": block(0, other), "aup": block(-1, x), "adn": block(1, x),
        "m1": block(1, other), "m2": block(-1, other), "m3": block(2, x), "m4": block(2, other),
    }
    return cross, up, down, order


def tp_gather(piece):
    width = piece.shape[1]
    half, quarter = width // 2, width // 4
    cross, up, down, order = tp_links(width)
    send = lambda value, perm: lax.ppermute(value, "tp", perm)
    ax = send(piece, cross)
    aup = send(piece, up)
    adn = send(piece, down)
    bx = send(jnp.concatenate([adn[:, :half], aup[:, :half]], 1), cross)
    bdn = send(jnp.concatenate([ax[:, half:], adn[:, :half]], 1), down)
    bup = send(jnp.concatenate([ax[:, half:], aup[:, half:]], 1), up)
    m1 = jnp.concatenate([bx[:, :half], bdn[:, :half]], 1)
    m2 = jnp.concatenate([bx[:, half:], bup[:, :half]], 1)
    m3 = jnp.concatenate([bdn[:, half:], bup[:, half:]], 1)
    cdn = send(m1[:, :half], down)
    cup = send(m2[:, half:], up)
    m4 = jnp.concatenate([cdn, cup], 1)
    return [[piece, ax, aup, adn], [m1, m2, m3], [m4]], order


def tp_reduce_scatter(b, width):
    half, quarter = width // 2, width // 4
    cross, up, down, order = tp_links(width)
    send = lambda value, perm: lax.ppermute(value.astype(jnp.bfloat16), "tp", perm).astype(jnp.float32)
    rup = send(b["m4"][:, :half], up)
    rdn = send(b["m4"][:, half:], down)
    m1, m2, m3 = b["m1"], b["m2"], b["m3"]
    m1 = jnp.concatenate([m1[:, :half] + rup, m1[:, half:]], 1)
    m2 = jnp.concatenate([m2[:, :half], m2[:, half:] + rdn], 1)
    rx = send(jnp.concatenate([m1[:, :half], m2[:, :half]], 1), cross)
    rup = send(jnp.concatenate([m1[:, half:], m3[:, :half]], 1), up)
    rdn = send(jnp.concatenate([m2[:, half:], m3[:, half:]], 1), down)
    ax = jnp.concatenate([b["ax"][:, :half], b["ax"][:, half:] + rup[:, :half] + rdn[:, :half]], 1)
    adn = jnp.concatenate([b["adn"][:, :half] + rx[:, :half] + rup[:, half:], b["adn"][:, half:]], 1)
    aup = jnp.concatenate([b["aup"][:, :half] + rx[:, half:], b["aup"][:, half:] + rdn[:, half:]], 1)
    return b["own"] + send(ax, cross) + send(adn, up) + send(aup, down)


def tp_sum(values):
    size = 8
    column = values
    for shift in (2, -2, 4):
        column = column + lax.ppermute(values, "tp", [(i, (i + shift) % size) for i in range(size)])
    return column + lax.ppermute(column, "tp", [(i, i ^ 1) for i in range(size)])


def rope_pack(proj, square, gains, cosine, sine, seqs, pos_dev, full_width):
    _, rows, width = proj.shape
    heads = width // HD

    def kernel(proj_ref, square_ref, gain_ref, cos_ref, sin_ref, pack_ref, fresh_ref):
        cos_v = cos_ref[...]
        sin_v = sin_ref[...]
        for c in range(3):
            x = proj_ref[c]
            if c < 2:
                x = x * lax.rsqrt(square_ref[c] / full_width + norm_eps) * gain_ref[c]
            for h in range(heads):
                xh = x[:, h * HD:(h + 1) * HD]
                if c < 2:
                    xh = xh * cos_v + pltpu.roll(xh, HD // 2, 1) * sin_v
                xh = xh.astype(jnp.bfloat16)
                for b in range(seqs):
                    pack_ref[b * heads + h, c] = xh[b * pos_dev:(b + 1) * pos_dev]
                fresh_ref[c, :, h * HD:(h + 1) * HD] = xh[seqs * pos_dev:].astype(jnp.float32)

    return pl.pallas_call(
        kernel,
        out_shape=(
            jax.ShapeDtypeStruct((seqs * heads, 3, pos_dev, HD), jnp.bfloat16),
            jax.ShapeDtypeStruct((3, rows - seqs * pos_dev, width), jnp.float32),
        ),
    )(proj, square, gains, cosine, sine)


def attend_pair(q_all, k_all, v_all, q_new, k_new, v_new, length):
    count = q_all.shape[0]
    scale = HD ** (-0.5)
    bounds = (0, count // 2, count * 3 // 4, count)
    outs = []
    for begin, stop in zip(bounds[:-1], bounds[1:]):
        scores = (
            jnp.dot(q_all[begin:stop], k_all[:stop].T, preferred_element_type=jnp.float32)
            * scale
        )
        query_pos = begin + jnp.arange(stop - begin, dtype=jnp.int32)[:, None]
        key_pos = jnp.arange(stop, dtype=jnp.int32)[None, :]
        valid = (key_pos <= query_pos) & (key_pos < length)
        scores = jnp.where(valid, scores, masked_fill)
        top = jnp.max(scores, -1, keepdims=True)
        weights = jnp.where(valid, jnp.exp(scores - top), 0.0)
        total = jnp.sum(weights, -1, keepdims=True)
        outs.append(
            jnp.dot(weights.astype(jnp.bfloat16), v_all[:stop], preferred_element_type=jnp.float32)
            / total
        )
    prompt_out = jnp.concatenate(outs, 0).astype(jnp.bfloat16)
    new_scores = jnp.dot(k_all, q_new, preferred_element_type=jnp.float32) * scale
    live = jnp.arange(count, dtype=jnp.int32) < length
    new_scores = jnp.where(live, new_scores, masked_fill)
    self_score = jnp.dot(q_new, k_new, preferred_element_type=jnp.float32) * scale
    new_top = jnp.maximum(jnp.max(new_scores), self_score)
    new_weights = jnp.where(live, jnp.exp(new_scores - new_top), 0.0)
    own_weight = jnp.exp(self_score - new_top)
    new_total = jnp.sum(new_weights) + own_weight
    own_rounded = lax.optimization_barrier(own_weight.astype(jnp.bfloat16)).astype(jnp.float32)
    numer = jnp.dot(new_weights.astype(jnp.bfloat16), v_all, preferred_element_type=jnp.float32)
    numer = numer + own_rounded * v_new.astype(jnp.float32)
    return prompt_out, (numer / new_total).astype(jnp.bfloat16)


def body(tokens, new_tokens, w_qkv, w_out, q_gain, k_gain, post_gain, lengths):
    seqs, pos_dev, width_local = tokens.shape
    heads_local = width_local // HD
    full_width = w_qkv.shape[1]
    n_seq = lax.axis_size("seq")
    pairs = seqs * heads_local
    assert pairs == n_seq
    prompt_rows = seqs * pos_dev
    full_len = pos_dev * n_seq
    flat_rows = tokens.reshape(prompt_rows, width_local)
    local_rows = jnp.concatenate([flat_rows, new_tokens], 0)
    rounds, order = tp_gather(local_rows)

    def in_relative_order(weight, axis):
        return [
            lax.dynamic_slice_in_dim(weight, order[name] * width_local, width_local, axis)
            for name in RELATIVE
        ]

    w_blocks = in_relative_order(w_qkv, 1)
    proj, start = None, 0
    for blocks in rounds:
        stop = start + len(blocks)
        term = jnp.einsum(
            "tn,cnf->ctf",
            jnp.concatenate(blocks, 1),
            jnp.concatenate(w_blocks[start:stop], 1),
            preferred_element_type=jnp.float32,
        )
        proj = term if proj is None else proj + term
        start = stop
    query_raw, key_raw = proj[0], proj[1]
    squares = tp_sum(jnp.stack([jnp.sum(query_raw * query_raw, -1), jnp.sum(key_raw * key_raw, -1)]))

    seq_index = lax.axis_index("seq")
    query_pos = seq_index * pos_dev + jnp.arange(pos_dev, dtype=jnp.int32)
    row_pos = jnp.concatenate([jnp.tile(query_pos, seqs), lengths.astype(jnp.int32)], 0)
    half = HD // 2
    freq = rope_base ** (-(jnp.arange(half, dtype=jnp.float32) * 2.0) / HD)
    angle = row_pos.astype(jnp.float32)[:, None] * freq
    cosine, sine = jnp.cos(angle), jnp.sin(angle)
    qkv, fresh = rope_pack(
        proj,
        squares[:, :, None],
        jnp.stack([q_gain, k_gain])[:, None, :],
        jnp.concatenate([cosine, cosine], 1),
        jnp.concatenate([-sine, sine], 1),
        seqs,
        pos_dev,
        full_width,
    )

    got = lax.all_to_all(qkv, "seq", 0, 0, tiled=True)
    full = got.transpose(1, 0, 2, 3).reshape(3, full_len, HD)

    owner = seq_index
    own_prompt = owner // heads_local
    fresh = fresh.astype(jnp.bfloat16).reshape(3, pairs, HD)
    new_q, new_k, new_v = fresh[0, owner], fresh[1, owner], fresh[2, owner]
    prompt_out, new_out = attend_pair(
        full[0], full[1], full[2], new_q, new_k, new_v, lengths[own_prompt]
    )

    pad = 8
    back = jnp.concatenate(
        [prompt_out.reshape(n_seq, pos_dev, HD), jnp.broadcast_to(new_out, (n_seq, pad, HD))], 1
    )
    ret = lax.all_to_all(back, "seq", 0, 0, tiled=True)
    ret = ret.reshape(seqs, heads_local, pos_dev + pad, HD)
    attn_rows = ret[:, :, :pos_dev].transpose(0, 2, 1, 3).reshape(prompt_rows, width_local)
    attn_new = ret[:, :, pos_dev].reshape(seqs, width_local)
    attention = jnp.concatenate([attn_rows, attn_new], 0)

    wo_blocks = in_relative_order(w_out, 1)
    part = {}
    for names in (RELATIVE[7:], RELATIVE[4:7], RELATIVE[:4]):
        columns = [wo_blocks[RELATIVE.index(name)] for name in names]
        value = jnp.dot(attention, jnp.concatenate(columns, 1), preferred_element_type=jnp.float32)
        for i, name in enumerate(names):
            part[name] = value[:, i * width_local:(i + 1) * width_local]
    summed = tp_reduce_scatter(part, width_local)
    square = tp_sum(jnp.sum(summed * summed, -1))
    out = (
        local_rows.astype(jnp.float32)
        + summed * lax.rsqrt(square[:, None] / full_width + norm_eps) * post_gain
    ).astype(jnp.bfloat16)
    return (
        out[:prompt_rows].reshape(seqs, pos_dev, width_local),
        out[prompt_rows:],
    )


def solution(mesh):
    in_specs = (
        P(None, "seq", "tp"),
        P(None, "tp"),
        P(None, None, "tp"),
        P("tp", None),
        P("tp"),
        P("tp"),
        P("tp"),
        P(),
    )
    out_specs = (P(None, "seq", "tp"), P(None, "tp"))
    return jax.shard_map(body, mesh=mesh, in_specs=in_specs, out_specs=out_specs, check_vma=False)
```

```python
import jax
import jax.numpy as jnp
from jax import lax
from jax.experimental import pallas as pl
from jax.experimental.pallas import tpu as pltpu
from jax.sharding import PartitionSpec as P

HD = 128


rope_base = 500000.0
norm_eps = 1e-06
masked_fill = -1e30


RELATIVE = ("own", "ax", "aup", "adn", "m1", "m2", "m3", "m4")


def tp_links(width):
    size = 8
    cross = [(i, i ^ 1) for i in range(size)]
    up = [(i, (i + 2) % size) for i in range(size)]
    down = [(i, (i - 2) % size) for i in range(size)]
    t = lax.axis_index("tp")
    y, x = t // 2, t % 2
    other = 1 - x

    def block(dy, side):
        return ((y + dy) % 4) * 2 + side

    order = {
        "own": block(0, x), "ax": block(0, other), "aup": block(-1, x), "adn": block(1, x),
        "m1": block(1, other), "m2": block(-1, other), "m3": block(2, x), "m4": block(2, other),
    }
    return cross, up, down, order


def tp_gather(piece):
    width = piece.shape[1]
    half, quarter = width // 2, width // 4
    cross, up, down, order = tp_links(width)
    send = lambda value, perm: lax.ppermute(value, "tp", perm)
    ax = send(piece, cross)
    aup = send(piece, up)
    adn = send(piece, down)
    bx = send(jnp.concatenate([adn[:, :half], aup[:, :half]], 1), cross)
    bdn = send(jnp.concatenate([ax[:, half:], adn[:, :half]], 1), down)
    bup = send(jnp.concatenate([ax[:, half:], aup[:, half:]], 1), up)
    m1 = jnp.concatenate([bx[:, :half], bdn[:, :half]], 1)
    m2 = jnp.concatenate([bx[:, half:], bup[:, :half]], 1)
    m3 = jnp.concatenate([bdn[:, half:], bup[:, half:]], 1)
    cdn = send(m1[:, :half], down)
    cup = send(m2[:, half:], up)
    m4 = jnp.concatenate([cdn, cup], 1)
    return [[piece, ax, aup, adn], [m1, m2, m3], [m4]], order


def tp_reduce_scatter(b, width):
    half, quarter = width // 2, width // 4
    cross, up, down, order = tp_links(width)
    send = lambda value, perm: lax.ppermute(value.astype(jnp.bfloat16), "tp", perm).astype(jnp.float32)
    rup = send(b["m4"][:, :half], up)
    rdn = send(b["m4"][:, half:], down)
    m1, m2, m3 = b["m1"], b["m2"], b["m3"]
    m1 = jnp.concatenate([m1[:, :half] + rup, m1[:, half:]], 1)
    m2 = jnp.concatenate([m2[:, :half], m2[:, half:] + rdn], 1)
    rx = send(jnp.concatenate([m1[:, :half], m2[:, :half]], 1), cross)
    rup = send(jnp.concatenate([m1[:, half:], m3[:, :half]], 1), up)
    rdn = send(jnp.concatenate([m2[:, half:], m3[:, half:]], 1), down)
    ax = jnp.concatenate([b["ax"][:, :half], b["ax"][:, half:] + rup[:, :half] + rdn[:, :half]], 1)
    adn = jnp.concatenate([b["adn"][:, :half] + rx[:, :half] + rup[:, half:], b["adn"][:, half:]], 1)
    aup = jnp.concatenate([b["aup"][:, :half] + rx[:, half:], b["aup"][:, half:] + rdn[:, half:]], 1)
    return b["own"] + send(ax, cross) + send(adn, up) + send(aup, down)


def tp_sum(values):
    size = 8
    column = values
    for shift in (2, -2, 4):
        column = column + lax.ppermute(values, "tp", [(i, (i + shift) % size) for i in range(size)])
    return column + lax.ppermute(column, "tp", [(i, i ^ 1) for i in range(size)])


def rope_pack(proj, square, gains, cosine, sine, seqs, pos_dev, full_width):
    _, rows, width = proj.shape
    heads = width // HD

    def kernel(proj_ref, square_ref, gain_ref, cos_ref, sin_ref, pack_ref, fresh_ref):
        cos_v = cos_ref[...]
        sin_v = sin_ref[...]
        for c in range(3):
            x = proj_ref[c]
            if c < 2:
                x = x * lax.rsqrt(square_ref[c] / full_width + norm_eps) * gain_ref[c]
            for h in range(heads):
                xh = x[:, h * HD:(h + 1) * HD]
                if c < 2:
                    xh = xh * cos_v + pltpu.roll(xh, HD // 2, 1) * sin_v
                xh = xh.astype(jnp.bfloat16)
                for b in range(seqs):
                    pack_ref[b * heads + h, c] = xh[b * pos_dev:(b + 1) * pos_dev]
                fresh_ref[c, :, h * HD:(h + 1) * HD] = xh[seqs * pos_dev:].astype(jnp.float32)

    return pl.pallas_call(
        kernel,
        out_shape=(
            jax.ShapeDtypeStruct((seqs * heads, 3, pos_dev, HD), jnp.bfloat16),
            jax.ShapeDtypeStruct((3, rows - seqs * pos_dev, width), jnp.float32),
        ),
    )(proj, square, gains, cosine, sine)


def attend_pair(q_all, k_all, v_all, q_new, k_new, v_new, length):
    count = q_all.shape[0]
    scale = HD ** (-0.5)
    bounds = (0, count * 7 // 16, count * 3 // 4, count)
    outs = []
    for begin, stop in zip(bounds[:-1], bounds[1:]):
        scores = (
            jnp.dot(q_all[begin:stop], k_all[:stop].T, preferred_element_type=jnp.float32)
            * scale
        )
        query_pos = begin + jnp.arange(stop - begin, dtype=jnp.int32)[:, None]
        key_pos = jnp.arange(stop, dtype=jnp.int32)[None, :]
        valid = (key_pos <= query_pos) & (key_pos < length)
        scores = jnp.where(valid, scores, masked_fill)
        top = jnp.max(scores, -1, keepdims=True)
        weights = jnp.where(valid, jnp.exp(scores - top), 0.0)
        total = jnp.sum(weights, -1, keepdims=True)
        outs.append(
            jnp.dot(weights.astype(jnp.bfloat16), v_all[:stop], preferred_element_type=jnp.float32)
            / total
        )
    prompt_out = jnp.concatenate(outs, 0).astype(jnp.bfloat16)
    new_scores = jnp.dot(k_all, q_new, preferred_element_type=jnp.float32) * scale
    live = jnp.arange(count, dtype=jnp.int32) < length
    new_scores = jnp.where(live, new_scores, masked_fill)
    self_score = jnp.dot(q_new, k_new, preferred_element_type=jnp.float32) * scale
    new_top = jnp.maximum(jnp.max(new_scores), self_score)
    new_weights = jnp.where(live, jnp.exp(new_scores - new_top), 0.0)
    own_weight = jnp.exp(self_score - new_top)
    new_total = jnp.sum(new_weights) + own_weight
    own_rounded = lax.optimization_barrier(own_weight.astype(jnp.bfloat16)).astype(jnp.float32)
    numer = jnp.dot(new_weights.astype(jnp.bfloat16), v_all, preferred_element_type=jnp.float32)
    numer = numer + own_rounded * v_new.astype(jnp.float32)
    return prompt_out, (numer / new_total).astype(jnp.bfloat16)


def body(tokens, new_tokens, w_qkv, w_out, q_gain, k_gain, post_gain, lengths):
    seqs, pos_dev, width_local = tokens.shape
    heads_local = width_local // HD
    full_width = w_qkv.shape[1]
    n_seq = lax.axis_size("seq")
    pairs = seqs * heads_local
    assert pairs == n_seq
    prompt_rows = seqs * pos_dev
    full_len = pos_dev * n_seq
    flat_rows = tokens.reshape(prompt_rows, width_local)
    local_rows = jnp.concatenate([flat_rows, new_tokens], 0)
    rounds, order = tp_gather(local_rows)

    def in_relative_order(weight, axis):
        return [
            lax.dynamic_slice_in_dim(weight, order[name] * width_local, width_local, axis)
            for name in RELATIVE
        ]

    w_blocks = in_relative_order(w_qkv, 1)
    proj, start = None, 0
    for blocks in rounds:
        stop = start + len(blocks)
        term = jnp.einsum(
            "tn,cnf->ctf",
            jnp.concatenate(blocks, 1),
            jnp.concatenate(w_blocks[start:stop], 1),
            preferred_element_type=jnp.float32,
        )
        proj = term if proj is None else proj + term
        start = stop
    query_raw, key_raw = proj[0], proj[1]
    squares = tp_sum(jnp.stack([jnp.sum(query_raw * query_raw, -1), jnp.sum(key_raw * key_raw, -1)]))

    seq_index = lax.axis_index("seq")
    query_pos = seq_index * pos_dev + jnp.arange(pos_dev, dtype=jnp.int32)
    row_pos = jnp.concatenate([jnp.tile(query_pos, seqs), lengths.astype(jnp.int32)], 0)
    half = HD // 2
    freq = rope_base ** (-(jnp.arange(half, dtype=jnp.float32) * 2.0) / HD)
    angle = row_pos.astype(jnp.float32)[:, None] * freq
    cosine, sine = jnp.cos(angle), jnp.sin(angle)
    qkv, fresh = rope_pack(
        proj,
        squares[:, :, None],
        jnp.stack([q_gain, k_gain])[:, None, :],
        jnp.concatenate([cosine, cosine], 1),
        jnp.concatenate([-sine, sine], 1),
        seqs,
        pos_dev,
        full_width,
    )

    got = lax.all_to_all(qkv, "seq", 0, 0, tiled=True)
    full = got.transpose(1, 0, 2, 3).reshape(3, full_len, HD)

    owner = seq_index
    own_prompt = owner // heads_local
    fresh = fresh.astype(jnp.bfloat16).reshape(3, pairs, HD)
    new_q, new_k, new_v = fresh[0, owner], fresh[1, owner], fresh[2, owner]
    prompt_out, new_out = attend_pair(
        full[0], full[1], full[2], new_q, new_k, new_v, lengths[own_prompt]
    )

    pad = 8
    back = jnp.concatenate(
        [prompt_out.reshape(n_seq, pos_dev, HD), jnp.broadcast_to(new_out, (n_seq, pad, HD))], 1
    )
    ret = lax.all_to_all(back, "seq", 0, 0, tiled=True)
    ret = ret.reshape(seqs, heads_local, pos_dev + pad, HD)
    attn_rows = ret[:, :, :pos_dev].transpose(0, 2, 1, 3).reshape(prompt_rows, width_local)
    attn_new = ret[:, :, pos_dev].reshape(seqs, width_local)
    attention = jnp.concatenate([attn_rows, attn_new], 0)

    wo_blocks = in_relative_order(w_out, 1)
    part = {}
    for names in (RELATIVE[7:], RELATIVE[4:7], RELATIVE[:4]):
        columns = [wo_blocks[RELATIVE.index(name)] for name in names]
        value = jnp.dot(attention, jnp.concatenate(columns, 1), preferred_element_type=jnp.float32)
        for i, name in enumerate(names):
            part[name] = value[:, i * width_local:(i + 1) * width_local]
    summed = tp_reduce_scatter(part, width_local)
    square = tp_sum(jnp.sum(summed * summed, -1))
    out = (
        local_rows.astype(jnp.float32)
        + summed * lax.rsqrt(square[:, None] / full_width + norm_eps) * post_gain
    ).astype(jnp.bfloat16)
    return (
        out[:prompt_rows].reshape(seqs, pos_dev, width_local),
        out[prompt_rows:],
    )


def solution(mesh):
    in_specs = (
        P(None, "seq", "tp"),
        P(None, "tp"),
        P(None, None, "tp"),
        P("tp", None),
        P("tp"),
        P("tp"),
        P("tp"),
        P(),
    )
    out_specs = (P(None, "seq", "tp"), P(None, "tp"))
    return jax.shard_map(body, mesh=mesh, in_specs=in_specs, out_specs=out_specs, check_vma=False)
```

```python
import jax
import jax.numpy as jnp
from jax import lax
from jax.experimental import pallas as pl
from jax.experimental.pallas import tpu as pltpu
from jax.sharding import PartitionSpec as P

HD = 128


rope_base = 500000.0
norm_eps = 1e-06
masked_fill = -1e30


RELATIVE = ("own", "ax", "aup", "adn", "m1", "m2", "m3", "m4")


def tp_links(width):
    size = 8
    cross = [(i, i ^ 1) for i in range(size)]
    up = [(i, (i + 2) % size) for i in range(size)]
    down = [(i, (i - 2) % size) for i in range(size)]
    t = lax.axis_index("tp")
    y, x = t // 2, t % 2
    other = 1 - x

    def block(dy, side):
        return ((y + dy) % 4) * 2 + side

    order = {
        "own": block(0, x), "ax": block(0, other), "aup": block(-1, x), "adn": block(1, x),
        "m1": block(1, other), "m2": block(-1, other), "m3": block(2, x), "m4": block(2, other),
    }
    return cross, up, down, order


def tp_gather(piece):
    width = piece.shape[1]
    half, quarter = width // 2, width // 4
    cross, up, down, order = tp_links(width)
    send = lambda value, perm: lax.ppermute(value, "tp", perm)
    ax = send(piece, cross)
    aup = send(piece, up)
    adn = send(piece, down)
    bx = send(jnp.concatenate([adn[:, :half], aup[:, :half]], 1), cross)
    bdn = send(jnp.concatenate([ax[:, half:], adn[:, :half]], 1), down)
    bup = send(jnp.concatenate([ax[:, half:], aup[:, half:]], 1), up)
    m1 = jnp.concatenate([bx[:, :half], bdn[:, :half]], 1)
    m2 = jnp.concatenate([bx[:, half:], bup[:, :half]], 1)
    m3 = jnp.concatenate([bdn[:, half:], bup[:, half:]], 1)
    cdn = send(m1[:, :half], down)
    cup = send(m2[:, half:], up)
    m4 = jnp.concatenate([cdn, cup], 1)
    return [[piece, ax, aup, adn], [m1, m2, m3], [m4]], order


def tp_reduce_scatter(b, width):
    half, quarter = width // 2, width // 4
    cross, up, down, order = tp_links(width)
    send = lambda value, perm: lax.ppermute(value.astype(jnp.bfloat16), "tp", perm).astype(jnp.float32)
    rup = send(b["m4"][:, :half], up)
    rdn = send(b["m4"][:, half:], down)
    m1, m2, m3 = b["m1"], b["m2"], b["m3"]
    m1 = jnp.concatenate([m1[:, :half] + rup, m1[:, half:]], 1)
    m2 = jnp.concatenate([m2[:, :half], m2[:, half:] + rdn], 1)
    rx = send(jnp.concatenate([m1[:, :half], m2[:, :half]], 1), cross)
    rup = send(jnp.concatenate([m1[:, half:], m3[:, :half]], 1), up)
    rdn = send(jnp.concatenate([m2[:, half:], m3[:, half:]], 1), down)
    ax = jnp.concatenate([b["ax"][:, :half], b["ax"][:, half:] + rup[:, :half] + rdn[:, :half]], 1)
    adn = jnp.concatenate([b["adn"][:, :half] + rx[:, :half] + rup[:, half:], b["adn"][:, half:]], 1)
    aup = jnp.concatenate([b["aup"][:, :half] + rx[:, half:], b["aup"][:, half:] + rdn[:, half:]], 1)
    return b["own"] + send(ax, cross) + send(adn, up) + send(aup, down)


def tp_sum(values):
    size = 8
    column = values
    for shift in (2, -2, 4):
        column = column + lax.ppermute(values, "tp", [(i, (i + shift) % size) for i in range(size)])
    return column + lax.ppermute(column, "tp", [(i, i ^ 1) for i in range(size)])


def rope_pack(proj, square, gains, cosine, sine, seqs, pos_dev, full_width):
    _, rows, width = proj.shape
    heads = width // HD

    def kernel(proj_ref, square_ref, gain_ref, cos_ref, sin_ref, pack_ref, fresh_ref):
        cos_v = cos_ref[...]
        sin_v = sin_ref[...]
        for c in range(3):
            x = proj_ref[c]
            if c < 2:
                x = x * lax.rsqrt(square_ref[c] / full_width + norm_eps) * gain_ref[c]
            for h in range(heads):
                xh = x[:, h * HD:(h + 1) * HD]
                if c < 2:
                    xh = xh * cos_v + pltpu.roll(xh, HD // 2, 1) * sin_v
                xh = xh.astype(jnp.bfloat16)
                for b in range(seqs):
                    pack_ref[b * heads + h, c] = xh[b * pos_dev:(b + 1) * pos_dev]
                fresh_ref[c, :, h * HD:(h + 1) * HD] = xh[seqs * pos_dev:]

    return pl.pallas_call(
        kernel,
        out_shape=(
            jax.ShapeDtypeStruct((seqs * heads, 3, pos_dev, HD), jnp.bfloat16),
            jax.ShapeDtypeStruct((3, rows - seqs * pos_dev, width), jnp.bfloat16),
        ),
    )(proj, square, gains, cosine, sine)


def attend_pair(q_all, k_all, v_all, q_new, k_new, v_new, length):
    count = q_all.shape[0]
    scale = HD ** (-0.5)
    bounds = (0, count * 7 // 16, count * 3 // 4, count)
    outs = []
    for begin, stop in zip(bounds[:-1], bounds[1:]):
        scores = (
            jnp.dot(q_all[begin:stop], k_all[:stop].T, preferred_element_type=jnp.float32)
            * scale
        )
        query_pos = begin + jnp.arange(stop - begin, dtype=jnp.int32)[:, None]
        key_pos = jnp.arange(stop, dtype=jnp.int32)[None, :]
        valid = (key_pos <= query_pos) & (key_pos < length)
        scores = jnp.where(valid, scores, masked_fill)
        top = jnp.max(scores, -1, keepdims=True)
        weights = jnp.where(valid, jnp.exp(scores - top), 0.0)
        total = jnp.sum(weights, -1, keepdims=True)
        outs.append(
            jnp.dot(weights.astype(jnp.bfloat16), v_all[:stop], preferred_element_type=jnp.float32)
            / total
        )
    prompt_out = jnp.concatenate(outs, 0).astype(jnp.bfloat16)
    new_scores = jnp.dot(k_all, q_new, preferred_element_type=jnp.float32) * scale
    live = jnp.arange(count, dtype=jnp.int32) < length
    new_scores = jnp.where(live, new_scores, masked_fill)
    self_score = jnp.dot(q_new, k_new, preferred_element_type=jnp.float32) * scale
    new_top = jnp.maximum(jnp.max(new_scores), self_score)
    new_weights = jnp.where(live, jnp.exp(new_scores - new_top), 0.0)
    own_weight = jnp.exp(self_score - new_top)
    new_total = jnp.sum(new_weights) + own_weight
    own_rounded = lax.optimization_barrier(own_weight.astype(jnp.bfloat16)).astype(jnp.float32)
    numer = jnp.dot(new_weights.astype(jnp.bfloat16), v_all, preferred_element_type=jnp.float32)
    numer = numer + own_rounded * v_new.astype(jnp.float32)
    return prompt_out, (numer / new_total).astype(jnp.bfloat16)


def body(tokens, new_tokens, w_qkv, w_out, q_gain, k_gain, post_gain, lengths):
    seqs, pos_dev, width_local = tokens.shape
    heads_local = width_local // HD
    full_width = w_qkv.shape[1]
    n_seq = lax.axis_size("seq")
    pairs = seqs * heads_local
    assert pairs == n_seq
    prompt_rows = seqs * pos_dev
    full_len = pos_dev * n_seq
    flat_rows = tokens.reshape(prompt_rows, width_local)
    local_rows = jnp.concatenate([flat_rows, new_tokens], 0)
    rounds, order = tp_gather(local_rows)

    def in_relative_order(weight, axis):
        return [
            lax.dynamic_slice_in_dim(weight, order[name] * width_local, width_local, axis)
            for name in RELATIVE
        ]

    w_blocks = in_relative_order(w_qkv, 1)
    proj, start = None, 0
    for blocks in rounds:
        stop = start + len(blocks)
        term = jnp.einsum(
            "tn,cnf->ctf",
            jnp.concatenate(blocks, 1),
            jnp.concatenate(w_blocks[start:stop], 1),
            preferred_element_type=jnp.float32,
        )
        proj = term if proj is None else proj + term
        start = stop
    query_raw, key_raw = proj[0], proj[1]
    squares = tp_sum(jnp.stack([jnp.sum(query_raw * query_raw, -1), jnp.sum(key_raw * key_raw, -1)]))

    seq_index = lax.axis_index("seq")
    query_pos = seq_index * pos_dev + jnp.arange(pos_dev, dtype=jnp.int32)
    row_pos = jnp.concatenate([jnp.tile(query_pos, seqs), lengths.astype(jnp.int32)], 0)
    half = HD // 2
    freq = rope_base ** (-(jnp.arange(half, dtype=jnp.float32) * 2.0) / HD)
    angle = row_pos.astype(jnp.float32)[:, None] * freq
    cosine, sine = jnp.cos(angle), jnp.sin(angle)
    qkv, fresh = rope_pack(
        proj,
        squares[:, :, None],
        jnp.stack([q_gain, k_gain])[:, None, :],
        jnp.concatenate([cosine, cosine], 1),
        jnp.concatenate([-sine, sine], 1),
        seqs,
        pos_dev,
        full_width,
    )

    got = lax.all_to_all(qkv, "seq", 0, 0, tiled=True)
    full = got.transpose(1, 0, 2, 3).reshape(3, full_len, HD)

    owner = seq_index
    own_prompt = owner // heads_local
    fresh = fresh.reshape(3, pairs, HD)
    new_q, new_k, new_v = fresh[0, owner], fresh[1, owner], fresh[2, owner]
    prompt_out, new_out = attend_pair(
        full[0], full[1], full[2], new_q, new_k, new_v, lengths[own_prompt]
    )

    pad = 8
    back = jnp.concatenate(
        [prompt_out.reshape(n_seq, pos_dev, HD), jnp.broadcast_to(new_out, (n_seq, pad, HD))], 1
    )
    ret = lax.all_to_all(back, "seq", 0, 0, tiled=True)
    ret = ret.reshape(seqs, heads_local, pos_dev + pad, HD)
    attn_rows = ret[:, :, :pos_dev].transpose(0, 2, 1, 3).reshape(prompt_rows, width_local)
    attn_new = ret[:, :, pos_dev].reshape(seqs, width_local)
    attention = jnp.concatenate([attn_rows, attn_new], 0)

    wo_blocks = in_relative_order(w_out, 1)
    part = {}
    for names in (RELATIVE[7:], RELATIVE[4:7], RELATIVE[:4]):
        columns = [wo_blocks[RELATIVE.index(name)] for name in names]
        value = jnp.dot(attention, jnp.concatenate(columns, 1), preferred_element_type=jnp.float32)
        for i, name in enumerate(names):
            part[name] = value[:, i * width_local:(i + 1) * width_local]
    summed = tp_reduce_scatter(part, width_local)
    square = tp_sum(jnp.sum(summed * summed, -1))
    out = (
        local_rows.astype(jnp.float32)
        + summed * lax.rsqrt(square[:, None] / full_width + norm_eps) * post_gain
    ).astype(jnp.bfloat16)
    return (
        out[:prompt_rows].reshape(seqs, pos_dev, width_local),
        out[prompt_rows:],
    )


def solution(mesh):
    in_specs = (
        P(None, "seq", "tp"),
        P(None, "tp"),
        P(None, None, "tp"),
        P("tp", None),
        P("tp"),
        P("tp"),
        P("tp"),
        P(),
    )
    out_specs = (P(None, "seq", "tp"), P(None, "tp"))
    return jax.shard_map(body, mesh=mesh, in_specs=in_specs, out_specs=out_specs, check_vma=False)
```
